128 devices in a mesh: dp: 16 (over x, y), fsdp: 8 (over z, core).
Axes of the slice: x: 4, y: 4, z: 4, core: 2. Of those that a mesh axis runs over, the one named last changes fastest.
Arguments:
- page_embed: bfloat16 [81920, 2048], P(('dp', 'fsdp')), may hold values from -6 to 6
- page_slot: int32 [81920], P(('dp', 'fsdp')), may hold values from 0 to 10239, as said below
- doc_ids: int32 [128, 640], P(('dp', 'fsdp')), may hold values from 0 to 9, never falling along the last dimension, each value on 1 to 128 neighbouring positions
- qkv_weight: bfloat16 [3, 2048, 1024], P(None, 'fsdp'), may hold values from -0.125 to 0.125
- out_weight: bfloat16 [1024, 2048], P(None, 'fsdp'), may hold values from -0.1875 to 0.1875
- fig_slot: int32 [2048], P(('dp', 'fsdp')), may hold values from 0 to 639
- cap_slot: int32 [2048], P(('dp', 'fsdp')), may hold values from 0 to 639
- logit_scale: float32 [1], replicated, may hold values from 10 to 30
- loss_cotangent: float32 [2048], P(('dp', 'fsdp')), may hold values from 8 to 64
Outputs:
- page_grad: bfloat16 [81920, 2048], P(('dp', 'fsdp'))
- pair_loss: float32 [2048], P(('dp', 'fsdp'))
The draws below stay inside these ranges and needn't reach their ends.
Inputs may be any that keep to these rules, and one draw needn't show every extreme that they name: page_slot // 640 is the dp index of the owner and page_slot % 640 the slot there; within each group every slot is named by exactly one page; one device sends at most 50 pages to one owner, and every device sends exactly 50 to some owners. `doc_ids`: along a device's slots the document number never falls; each of the 10 documents has 1 to 128 slots, one exactly 128. `fig_slot`: a slot of the pair's own device. `cap_slot`: a slot of the pair's own device.
All inputs are finite; a program needn't handle non-finite values.
Results may differ from the reference program's by a relative error of at most 0.017.
Values may be sent and summed in bfloat16 or wider, within the bound.
No kernel may reach another device: no remote copies, remote signals or barrier semaphores. Data moves between devices by JAX's collectives and lax.ppermute only.
A program may use at most 192 MiB of HBM per device.

```python
import math
import jax
import jax.numpy as jnp
import numpy as np
from jax import lax

D = 2048
HD = 64
DOC_MAX = 128
PAGES_PER_DEVICE = 640
PAIRS_DEV = 16
HDIM = 1024
DOCS_DEV = 10
PAGES = 81920
PAIRS = 2048
N_DP = 16
N_FSDP = 8
DEVICES = 128


def draw_page_slot(key, part):
    dp_count = N_DP
    fsdp_count = N_FSDP
    page_count = PAGES_PER_DEVICE
    unit_count = page_count // (4 * dp_count)
    half_count = dp_count // 2

    def one_group(group_key):
        key_extra, key_shift, key_slots, key_order = jax.random.split(group_key, 4)
        extra_order = jax.random.permutation(key_extra, dp_count)
        extra = jnp.where(extra_order < half_count, 2 * unit_count, 0)
        shift = jax.random.randint(key_shift, (), 0, dp_count)
        source = jnp.arange(dp_count)[:, None]
        owner_col = jnp.arange(dp_count)[None, :]
        counts = 3 * unit_count + extra[(owner_col - source + shift) % dp_count]
        offsets = jnp.cumsum(counts, axis=0) - counts
        starts = jnp.cumsum(counts, axis=1) - counts
        slot_perm = jax.vmap(lambda sub_key: jax.random.permutation(sub_key, page_count))(jax.random.split(key_slots, dp_count))
        page_index = jnp.arange(page_count)
        owner_idx = jnp.sum((starts[:, None, :] <= page_index[None, :, None]).astype(jnp.int32), axis=2) - 1
        start_at = jnp.take_along_axis(starts, owner_idx, axis=1)
        offset_at = jnp.take_along_axis(offsets, owner_idx, axis=1)
        position = offset_at + page_index[None, :] - start_at
        chosen = slot_perm[owner_idx, position]
        global_slot = owner_idx * page_count + chosen
        page_order = jax.vmap(lambda sub_key: jax.random.permutation(sub_key, page_count))(jax.random.split(key_order, dp_count))
        return jnp.take_along_axis(global_slot, page_order, axis=1)
    groups = jax.vmap(one_group)(jax.random.split(jax.random.fold_in(key, 11), fsdp_count))
    return jnp.transpose(groups, (1, 0, 2)).reshape(-1).astype(jnp.int32)


def touch_ends(result, key, smallest, top_value):
    longest = result.shape.index(max(result.shape))
    spots = []
    for shift in (0, 1):
        where = [jax.random.randint(jax.random.fold_in(key, axis), (), 0, length) for axis, length in enumerate(result.shape)]
        where[longest] = (where[longest] + shift) % result.shape[longest]
        spots.append(tuple(where))
    return result.at[spots[0]].set(smallest).at[spots[1]].set(top_value)


def levels(own_key, extent, pieces, least, largest):
    loudness = 1.0
    for dim, shards_of in pieces:
        draws = jax.random.uniform(jax.random.fold_in(jax.random.fold_in(own_key, 6), dim), (shards_of,), jnp.float32, least / len(pieces), largest / len(pieces))
        loudness = loudness * jnp.repeat(jnp.exp(draws), extent[dim] // shards_of).reshape((-1,) + (1,) * (len(extent) - 1 - dim))
    return loudness


def length_profile(amount, total, reach, lean):
    loads = [(1 << 20) // math.isqrt(rank ** lean) + 1 for rank in range(2, amount + 1)]
    rest, holding = total - reach - (amount - 1), [1] * (amount - 1)
    while rest > 0:
        free = [i for i in range(amount - 1) if holding[i] < reach]
        whole, left = sum([loads[i] for i in free]), rest
        for i in free:
            more = min(reach - holding[i], max(1, left * loads[i] // whole), rest)
            holding[i] = holding[i] + more
            rest = rest - more
    return np.array([reach] + holding)


def uneven(own_key, amount, total, reach, slope):
    if amount == 2:
        one = jax.random.randint(own_key, (), max(1, total - reach), min(reach, total - 1) + 1)
        return jnp.stack([one, total - one])
    sizes = jnp.asarray(length_profile(amount, total, reach, slope), jnp.int32)
    couples = (amount - 1) // 2
    source_of, sink = sizes[1:1 + 2 * couples:2], sizes[2:2 + 2 * couples:2]
    room = jnp.minimum(source_of - 1, reach - sink)
    moved = jax.random.randint(jax.random.fold_in(own_key, 1), (couples,), 0, 1 << 20) % (room + 1)
    sizes = sizes.at[1:1 + 2 * couples:2].set(source_of - moved).at[2:2 + 2 * couples:2].set(sink + moved)
    return sizes[jax.random.permutation(jax.random.fold_in(own_key, 2), amount)]


def bell_draw(own_key, shape, width, limit, cuts=(), kind=jnp.bfloat16):
    array = width * jax.random.normal(own_key, shape, jnp.float32)
    if cuts:
        array = array * levels(own_key, shape, cuts, -0.22, 0.18)
    return jnp.clip(array, -limit, limit).astype(kind)


def setup_inputs(seed: int = 0) -> dict:
    streams_of = jax.random.split(jax.random.key(seed), 10)
    page_embed = bell_draw(streams_of[0], (PAGES, D), 1.0, 6.0, ((0, 128),))
    page_slot = draw_page_slot(jax.random.fold_in(streams_of[9], 71), 0)
    doc_ids = jax.vmap(lambda own: jnp.searchsorted(jnp.cumsum(uneven(own, DOCS_DEV, PAGES_PER_DEVICE, DOC_MAX, 1)), jnp.arange(PAGES_PER_DEVICE), side="right"))(jax.random.split(streams_of[2], DEVICES)).reshape((DEVICES, PAGES_PER_DEVICE)).astype(jnp.int32)
    qkv_weight = bell_draw(streams_of[3], (3, D, HDIM), D ** -0.5, 0.125, ((1, 8),))
    out_weight = bell_draw(streams_of[4], (HDIM, D), HDIM ** -0.5, 0.1875, ((1, 8),))
    fig_slot = touch_ends(jax.random.randint(streams_of[5], (PAIRS,), 0, PAGES_PER_DEVICE), jax.random.fold_in(streams_of[5], 1), 0, PAGES_PER_DEVICE - 1).astype(jnp.int32)
    cap_slot = touch_ends(jax.random.randint(streams_of[6], (PAIRS,), 0, PAGES_PER_DEVICE), jax.random.fold_in(streams_of[6], 1), 0, PAGES_PER_DEVICE - 1).astype(jnp.int32)
    logit_scale = jnp.clip(jax.random.uniform(streams_of[7], (1,), jnp.float32, 10.0, 30.0), 10.0, 30.0)
    loss_cotangent = jnp.clip(jnp.exp(math.log(64.0) - 2.0794415 * jax.random.uniform(streams_of[8], (PAIRS,), jnp.float32) ** levels(streams_of[8], (PAIRS,), ((0, 128),), -0.2, 0.2)), 8.0, 64.0)
    return {"page_embed": page_embed, "page_slot": page_slot, "doc_ids": doc_ids, "qkv_weight": qkv_weight, "out_weight": out_weight, "fig_slot": fig_slot, "cap_slot": cap_slot, "logit_scale": logit_scale, "loss_cotangent": loss_cotangent}


EPSILON = 1e-06

def log_total(values, axis):
    return jnp.log(lax.optimization_barrier(jnp.sum(jnp.exp(values), axis=axis)))

def attend(slot_row_block, qkv_mat, out_mat, doc_row):
    row_count = slot_row_block.shape[0]
    query_h = jnp.dot(slot_row_block, qkv_mat[0], preferred_element_type=jnp.float32).astype(jnp.bfloat16).reshape(row_count, -1, HD)
    key_h = jnp.dot(slot_row_block, qkv_mat[1], preferred_element_type=jnp.float32).astype(jnp.bfloat16).reshape(row_count, -1, HD)
    value_h = jnp.dot(slot_row_block, qkv_mat[2], preferred_element_type=jnp.float32).astype(jnp.bfloat16).reshape(row_count, -1, HD)
    scores = jnp.einsum('qhd,khd->hqk', query_h.astype(jnp.float32), key_h.astype(jnp.float32)) * (1.0 / math.sqrt(HD))
    same_doc = doc_row[:, None] == doc_row[None, :]
    scores = jnp.where(same_doc[None], scores, -1e+30)
    weights = jnp.exp(scores)
    attn_prob = (weights / lax.optimization_barrier(jnp.sum(weights, axis=2, keepdims=True))).astype(jnp.bfloat16)
    mixed = jnp.einsum('hqk,khd->qhd', attn_prob.astype(jnp.float32), value_h.astype(jnp.float32))
    mixed = mixed.astype(jnp.bfloat16).reshape(row_count, -1)
    return jnp.dot(mixed, out_mat, preferred_element_type=jnp.float32)

def reference(page_embed, page_slot, doc_ids, qkv_weight, out_weight, fig_slot, cap_slot, logit_scale, loss_cotangent):
    feature_width = page_embed.shape[1]
    group_pages = page_embed.reshape(N_DP, N_FSDP, PAGES_PER_DEVICE, feature_width).transpose(1, 0, 2, 3).reshape(N_FSDP, N_DP * PAGES_PER_DEVICE, feature_width)
    group_dest = page_slot.reshape(N_DP, N_FSDP, PAGES_PER_DEVICE).transpose(1, 0, 2).reshape(N_FSDP, N_DP * PAGES_PER_DEVICE)
    group_docs = doc_ids.reshape(N_DP, N_FSDP, PAGES_PER_DEVICE).transpose(1, 0, 2)
    group_fig = fig_slot.reshape(N_DP, N_FSDP, PAIRS_DEV).transpose(1, 0, 2)
    group_cap = cap_slot.reshape(N_DP, N_FSDP, PAIRS_DEV).transpose(1, 0, 2)
    group_weight = loss_cotangent.reshape(N_DP, N_FSDP, PAIRS_DEV).transpose(1, 0, 2)
    logit_mult = logit_scale[0]
    pair_total = N_DP * PAIRS_DEV

    def one_group(group_arguments):
        pages_gradient, destination_gradient, document_gradient, figure_gradient, caption_gradient, weight_gradient = group_arguments
        slot_row_block = jnp.zeros_like(pages_gradient).at[destination_gradient].set(pages_gradient).reshape(N_DP, PAGES_PER_DEVICE, feature_width)

        def forward_pass(entry_args):
            owner_rows, doc_row = entry_args
            return owner_rows.astype(jnp.float32) + attend(owner_rows, qkv_weight, out_weight, doc_row)
        slot_output = lax.map(forward_pass, (slot_row_block, document_gradient))
        fig_vec = jnp.take_along_axis(slot_output, figure_gradient[:, :, None], axis=1).reshape(pair_total, feature_width)
        cap_vec = jnp.take_along_axis(slot_output, caption_gradient[:, :, None], axis=1).reshape(pair_total, feature_width)
        fig_inv = lax.rsqrt(lax.optimization_barrier(jnp.sum(fig_vec * fig_vec, axis=1, keepdims=True)) + EPSILON)
        cap_inv = lax.rsqrt(lax.optimization_barrier(jnp.sum(cap_vec * cap_vec, axis=1, keepdims=True)) + EPSILON)
        fig_unit = fig_vec * fig_inv
        cap_unit = cap_vec * cap_inv
        fig_emb = fig_unit.astype(jnp.bfloat16)
        cap_emb = cap_unit.astype(jnp.bfloat16)
        logits = logit_mult * jnp.dot(fig_emb, cap_emb.T, preferred_element_type=jnp.float32)
        row_lse = log_total(logits, 1)
        col_lse = log_total(logits, 0)
        diag_logit = jnp.diagonal(logits)
        pair_loss = 0.5 * (row_lse - diag_logit) + 0.5 * (col_lse - diag_logit)
        eye_mat = jnp.eye(pair_total, dtype=jnp.float32)
        pair_weight = weight_gradient.reshape(-1)
        prob_rows = jnp.exp(logits - row_lse[:, None])
        prob_cols = jnp.exp(logits - col_lse[None, :])
        coef = 0.5 * pair_weight[:, None] * (prob_rows - eye_mat) + 0.5 * (prob_cols - eye_mat) * pair_weight[None, :]
        fig_grad = logit_mult * jnp.dot(coef, cap_emb.astype(jnp.float32), precision=lax.Precision.HIGHEST)
        cap_grad = logit_mult * jnp.dot(coef.T, fig_emb.astype(jnp.float32), precision=lax.Precision.HIGHEST)
        figure_direction = fig_inv * (fig_grad - fig_unit * lax.optimization_barrier(jnp.sum(fig_unit * fig_grad, axis=1, keepdims=True)))
        caption_direction = cap_inv * (cap_grad - cap_unit * lax.optimization_barrier(jnp.sum(cap_unit * cap_grad, axis=1, keepdims=True)))
        figure_direction = figure_direction.reshape(N_DP, PAIRS_DEV, feature_width)
        caption_direction = caption_direction.reshape(N_DP, PAIRS_DEV, feature_width)

        def backward_pass(entry_args):
            owner_rows, doc_row, fig_idx, cap_idx, fig_part, cap_part = entry_args
            slot_ct = jnp.zeros((PAGES_PER_DEVICE, feature_width), jnp.float32).at[fig_idx].add(fig_part).at[cap_idx].add(cap_part)

            def branch(inputs):
                return attend(inputs, qkv_weight, out_weight, doc_row)
            attn_out, pullback = jax.vjp(branch, owner_rows)
            branch_ct = pullback(slot_ct)[0]
            return (slot_ct + branch_ct.astype(jnp.float32)).astype(jnp.bfloat16)
        slot_gradient = lax.map(backward_pass, (slot_row_block, document_gradient, figure_gradient, caption_gradient, figure_direction, caption_direction)).reshape(N_DP * PAGES_PER_DEVICE, feature_width)
        return (slot_gradient[destination_gradient], pair_loss.reshape(N_DP, PAIRS_DEV))
    grads, losses = lax.map(one_group, (group_pages, group_dest, group_docs, group_fig, group_cap, group_weight))
    page_grad = grads.reshape(N_FSDP, N_DP, PAGES_PER_DEVICE, feature_width).transpose(1, 0, 2, 3).reshape(-1, feature_width)
    pair_loss = losses.transpose(1, 0, 2).reshape(-1)
    return (page_grad, pair_loss)
```

```python
import math

import jax
import jax.numpy as jnp
from jax import lax
from jax.sharding import PartitionSpec as P

HD = 64


EPSILON = 1e-06


def log_total(values, axis):
    return jnp.log(jnp.sum(jnp.exp(values), axis=axis))


def attend(slot_row_block, qkv_mat, out_mat, doc_row):
    row_count = slot_row_block.shape[0]
    query_h = (
        jnp.dot(slot_row_block, qkv_mat[0], preferred_element_type=jnp.float32)
        .astype(jnp.bfloat16)
        .reshape(row_count, -1, HD)
    )
    key_h = (
        jnp.dot(slot_row_block, qkv_mat[1], preferred_element_type=jnp.float32)
        .astype(jnp.bfloat16)
        .reshape(row_count, -1, HD)
    )
    value_h = (
        jnp.dot(slot_row_block, qkv_mat[2], preferred_element_type=jnp.float32)
        .astype(jnp.bfloat16)
        .reshape(row_count, -1, HD)
    )
    scores = jnp.einsum("qhd,khd->hqk", query_h, key_h, preferred_element_type=jnp.float32) * (
        1.0 / math.sqrt(HD)
    )
    same_doc = doc_row[:, None] == doc_row[None, :]
    scores = jnp.where(same_doc[None], scores, -1e30)
    weights = jnp.exp(scores)
    attn_prob = (weights / jnp.sum(weights, axis=2, keepdims=True)).astype(jnp.bfloat16)
    mixed = jnp.einsum("hqk,khd->qhd", attn_prob, value_h, preferred_element_type=jnp.float32)
    mixed = mixed.astype(jnp.bfloat16).reshape(row_count, -1)
    return jnp.dot(mixed, out_mat, preferred_element_type=jnp.float32)


def select_rows(onehot, rows):
    picked = jnp.dot(onehot, rows, preferred_element_type=jnp.float32)
    return picked.astype(rows.dtype)


def select_rows_t(onehot, rows):
    picked = lax.dot_general(
        onehot, rows, (((0,), (0,)), ((), ())), preferred_element_type=jnp.float32
    )
    return picked.astype(rows.dtype)


def body(
    page_embed,
    page_slot,
    doc_ids,
    qkv_weight,
    out_weight,
    fig_slot,
    cap_slot,
    logit_scale,
    loss_cotangent,
):
    dp_count = lax.axis_size("dp")
    row_count = page_embed.shape[0]
    feature_width = page_embed.shape[1]
    capacity = 5 * row_count // (4 * dp_count)
    buffer_rows = dp_count * capacity
    owner_idx = page_slot // row_count
    slot_idx = page_slot % row_count
    onehot = (owner_idx[:, None] == jnp.arange(dp_count)[None, :]).astype(jnp.int32)
    rank_idx = jnp.sum((jnp.cumsum(onehot, axis=0) - onehot) * onehot, axis=1)
    dest = owner_idx * capacity + rank_idx
    send_match = dest[None, :] == jnp.arange(buffer_rows)[:, None]
    send_onehot = send_match.astype(jnp.bfloat16)
    send_rows = select_rows(send_onehot, page_embed)
    send_ids = jnp.where(
        jnp.any(send_match, axis=1),
        jnp.sum(jnp.where(send_match, slot_idx[None, :], 0), axis=1),
        row_count,
    ).reshape(dp_count, capacity)
    recv_rows, recv_ids = (
        lax.all_to_all(
            send_rows.reshape(dp_count, capacity, feature_width),
            "dp",
            split_axis=0,
            concat_axis=0,
            tiled=True,
        ),
        lax.all_to_all(send_ids, "dp", split_axis=0, concat_axis=0, tiled=True),
    )
    flat_ids = recv_ids.reshape(-1)
    recv_onehot = (jnp.arange(row_count)[:, None] == flat_ids[None, :]).astype(jnp.bfloat16)
    slot_row_block = select_rows(recv_onehot, recv_rows.reshape(-1, feature_width))
    qkv_full, out_full = (
        lax.all_gather(qkv_weight, "fsdp", axis=1, tiled=True),
        lax.all_gather(out_weight, "fsdp", axis=1, tiled=True),
    )
    doc_row = doc_ids[0]

    def branch(inputs):
        return attend(inputs, qkv_full, out_full, doc_row)

    attn_out, pullback = jax.vjp(branch, slot_row_block)
    slot_output = slot_row_block.astype(jnp.float32) + attn_out
    fig_vec = slot_output[fig_slot]
    cap_vec = slot_output[cap_slot]
    fig_inv = lax.rsqrt(jnp.sum(fig_vec * fig_vec, axis=1, keepdims=True) + EPSILON)
    cap_inv = lax.rsqrt(jnp.sum(cap_vec * cap_vec, axis=1, keepdims=True) + EPSILON)
    fig_unit = fig_vec * fig_inv
    cap_unit = cap_vec * cap_inv
    fig_emb = fig_unit.astype(jnp.bfloat16)
    cap_emb = cap_unit.astype(jnp.bfloat16)
    pair_count = fig_slot.shape[0]
    both_emb = jnp.concatenate([fig_emb, cap_emb], axis=0)
    all_both = lax.all_gather(both_emb, "dp", axis=0, tiled=False)
    all_weight = lax.all_gather(loss_cotangent, "dp", axis=0, tiled=True)
    all_fig = all_both[:, :pair_count].reshape(-1, feature_width)
    all_cap = all_both[:, pair_count:].reshape(-1, feature_width)
    logit_mult = logit_scale[0]
    pair_total = all_fig.shape[0]
    first_pair = lax.axis_index("dp") * pair_count
    logits = logit_mult * jnp.dot(all_fig, all_cap.T, preferred_element_type=jnp.float32)
    row_lse = log_total(logits, 1)
    col_lse = log_total(logits, 0)
    eye_mat = jnp.eye(pair_total, dtype=jnp.float32)
    diag_logit = jnp.sum(logits * eye_mat, axis=1)
    own_rows = first_pair + jnp.arange(pair_count)
    own_mask = (jnp.arange(pair_total)[None, :] == own_rows[:, None]).astype(jnp.float32)
    loss_all = 0.5 * (row_lse - diag_logit) + 0.5 * (col_lse - diag_logit)
    pair_loss = jnp.dot(own_mask, loss_all, precision=lax.Precision.HIGHEST)
    prob_rows = jnp.exp(logits - row_lse[:, None])
    prob_cols = jnp.exp(logits - col_lse[None, :])
    coef = 0.5 * all_weight[:, None] * (prob_rows - eye_mat) + 0.5 * (
        prob_cols - eye_mat
    ) * all_weight[None, :]
    coef_rows = jnp.dot(own_mask, coef, precision=lax.Precision.HIGHEST)
    coef_cols = jnp.dot(own_mask, coef.T, precision=lax.Precision.HIGHEST)
    fig_grad = logit_mult * jnp.dot(
        coef_rows, all_cap.astype(jnp.float32), precision=lax.Precision.HIGHEST
    )
    cap_grad = logit_mult * jnp.dot(
        coef_cols, all_fig.astype(jnp.float32), precision=lax.Precision.HIGHEST
    )
    figure_direction = fig_inv * (
        fig_grad - fig_unit * jnp.sum(fig_unit * fig_grad, axis=1, keepdims=True)
    )
    caption_direction = cap_inv * (
        cap_grad - cap_unit * jnp.sum(cap_unit * cap_grad, axis=1, keepdims=True)
    )
    slot_ct = (
        jnp.zeros((row_count, feature_width), jnp.float32)
        .at[fig_slot]
        .add(figure_direction)
        .at[cap_slot]
        .add(caption_direction)
    )
    branch_ct = pullback(slot_ct)[0]
    slot_gradient = (slot_ct + branch_ct.astype(jnp.float32)).astype(jnp.bfloat16)
    back_rows = select_rows_t(recv_onehot, slot_gradient)
    home_rows = lax.all_to_all(
        back_rows.reshape(dp_count, capacity, feature_width),
        "dp",
        split_axis=0,
        concat_axis=0,
        tiled=True,
    )
    page_grad = select_rows_t(send_onehot, home_rows.reshape(-1, feature_width))
    return (page_grad, pair_loss)


def solution(mesh):
    return jax.shard_map(
        body,
        mesh=mesh,
        in_specs=(
            P(("dp", "fsdp"), None),
            P(("dp", "fsdp")),
            P(("dp", "fsdp"), None),
            P(None, "fsdp", None),
            P(None, "fsdp"),
            P(("dp", "fsdp")),
            P(("dp", "fsdp")),
            P(),
            P(("dp", "fsdp")),
        ),
        out_specs=(P(("dp", "fsdp"), None), P(("dp", "fsdp"))),
        check_vma=False,
    )
```

```python
import math

import jax
import jax.numpy as jnp
from jax import lax
from jax.sharding import PartitionSpec as P

HD = 64


EPSILON = 1e-06


def log_total(values, axis):
    return jnp.log(jnp.sum(jnp.exp(values), axis=axis))


def attend(slot_row_block, qkv_mat, out_mat, doc_row):
    row_count = slot_row_block.shape[0]
    query_h = (
        jnp.dot(slot_row_block, qkv_mat[0], preferred_element_type=jnp.float32)
        .astype(jnp.bfloat16)
        .reshape(row_count, -1, HD)
    )
    key_h = (
        jnp.dot(slot_row_block, qkv_mat[1], preferred_element_type=jnp.float32)
        .astype(jnp.bfloat16)
        .reshape(row_count, -1, HD)
    )
    value_h = (
        jnp.dot(slot_row_block, qkv_mat[2], preferred_element_type=jnp.float32)
        .astype(jnp.bfloat16)
        .reshape(row_count, -1, HD)
    )
    scores = jnp.einsum("qhd,khd->hqk", query_h, key_h, preferred_element_type=jnp.float32) * (
        1.0 / math.sqrt(HD)
    )
    same_doc = doc_row[:, None] == doc_row[None, :]
    scores = jnp.where(same_doc[None], scores, -1e30)
    weights = jnp.exp(scores)
    attn_prob = (weights / jnp.sum(weights, axis=2, keepdims=True)).astype(jnp.bfloat16)
    mixed = jnp.einsum("hqk,khd->qhd", attn_prob, value_h, preferred_element_type=jnp.float32)
    mixed = mixed.astype(jnp.bfloat16).reshape(row_count, -1)
    return jnp.dot(mixed, out_mat, preferred_element_type=jnp.float32)


def select_rows(onehot, rows):
    picked = jnp.dot(onehot, rows, preferred_element_type=jnp.float32)
    return picked.astype(rows.dtype)


def select_rows_t(onehot, rows):
    picked = lax.dot_general(
        onehot, rows, (((0,), (0,)), ((), ())), preferred_element_type=jnp.float32
    )
    return picked.astype(rows.dtype)


def body(
    page_embed,
    page_slot,
    doc_ids,
    qkv_weight,
    out_weight,
    fig_slot,
    cap_slot,
    logit_scale,
    loss_cotangent,
):
    dp_count = lax.axis_size("dp")
    row_count = page_embed.shape[0]
    feature_width = page_embed.shape[1]
    capacity = 5 * row_count // (4 * dp_count)
    buffer_rows = dp_count * capacity
    owner_idx = page_slot // row_count
    slot_idx = page_slot % row_count
    onehot = (owner_idx[:, None] == jnp.arange(dp_count)[None, :]).astype(jnp.int32)
    rank_idx = jnp.sum((jnp.cumsum(onehot, axis=0) - onehot) * onehot, axis=1)
    dest = owner_idx * capacity + rank_idx
    send_match = dest[None, :] == jnp.arange(buffer_rows)[:, None]
    send_onehot = send_match.astype(jnp.bfloat16)
    send_rows = select_rows(send_onehot, page_embed)
    send_ids = jnp.where(
        jnp.any(send_match, axis=1),
        jnp.sum(jnp.where(send_match, slot_idx[None, :], 0), axis=1),
        row_count,
    ).reshape(dp_count, capacity)
    recv_rows, recv_ids = (
        lax.all_to_all(
            send_rows.reshape(dp_count, capacity, feature_width),
            "dp",
            split_axis=0,
            concat_axis=0,
            tiled=True,
        ),
        lax.all_to_all(send_ids, "dp", split_axis=0, concat_axis=0, tiled=True),
    )
    flat_ids = recv_ids.reshape(-1)
    recv_onehot = (jnp.arange(row_count)[:, None] == flat_ids[None, :]).astype(jnp.bfloat16)
    slot_row_block = select_rows(recv_onehot, recv_rows.reshape(-1, feature_width))
    qkv_full, out_full = (
        lax.all_gather(qkv_weight, "fsdp", axis=1, tiled=True),
        lax.all_gather(out_weight, "fsdp", axis=1, tiled=True),
    )
    doc_row = doc_ids[0]

    def branch(inputs):
        return attend(inputs, qkv_full, out_full, doc_row)

    attn_out, pullback = jax.vjp(branch, slot_row_block)
    slot_output = slot_row_block.astype(jnp.float32) + attn_out
    fig_vec = slot_output[fig_slot]
    cap_vec = slot_output[cap_slot]
    fig_inv = lax.rsqrt(jnp.sum(fig_vec * fig_vec, axis=1, keepdims=True) + EPSILON)
    cap_inv = lax.rsqrt(jnp.sum(cap_vec * cap_vec, axis=1, keepdims=True) + EPSILON)
    fig_unit = fig_vec * fig_inv
    cap_unit = cap_vec * cap_inv
    fig_emb = fig_unit.astype(jnp.bfloat16)
    cap_emb = cap_unit.astype(jnp.bfloat16)
    pair_count = fig_slot.shape[0]
    weight_hi = loss_cotangent.astype(jnp.bfloat16)
    weight_lo = (loss_cotangent - weight_hi.astype(jnp.float32)).astype(jnp.bfloat16)
    weight_rows = jnp.zeros((2, feature_width), jnp.bfloat16)
    weight_rows = weight_rows.at[0, :pair_count].set(weight_hi).at[1, :pair_count].set(weight_lo)
    both_emb = jnp.concatenate([fig_emb, cap_emb, weight_rows], axis=0)
    all_both = lax.all_gather(both_emb, "dp", axis=0, tiled=False)
    all_fig = all_both[:, :pair_count].reshape(-1, feature_width)
    all_cap = all_both[:, pair_count : 2 * pair_count].reshape(-1, feature_width)
    all_weight = (
        all_both[:, 2 * pair_count, :pair_count].astype(jnp.float32)
        + all_both[:, 2 * pair_count + 1, :pair_count].astype(jnp.float32)
    ).reshape(-1)
    logit_mult = logit_scale[0]
    pair_total = all_fig.shape[0]
    first_pair = lax.axis_index("dp") * pair_count
    logits = logit_mult * jnp.dot(all_fig, all_cap.T, preferred_element_type=jnp.float32)
    row_lse = log_total(logits, 1)
    col_lse = log_total(logits, 0)
    eye_mat = jnp.eye(pair_total, dtype=jnp.float32)
    diag_logit = jnp.sum(logits * eye_mat, axis=1)
    own_rows = first_pair + jnp.arange(pair_count)
    own_mask = (jnp.arange(pair_total)[None, :] == own_rows[:, None]).astype(jnp.float32)
    loss_all = 0.5 * (row_lse - diag_logit) + 0.5 * (col_lse - diag_logit)
    pair_loss = jnp.dot(own_mask, loss_all, precision=lax.Precision.HIGHEST)
    prob_rows = jnp.exp(logits - row_lse[:, None])
    prob_cols = jnp.exp(logits - col_lse[None, :])
    coef = 0.5 * all_weight[:, None] * (prob_rows - eye_mat) + 0.5 * (
        prob_cols - eye_mat
    ) * all_weight[None, :]
    coef_rows = jnp.dot(own_mask, coef, precision=lax.Precision.HIGHEST)
    coef_cols = jnp.dot(own_mask, coef.T, precision=lax.Precision.HIGHEST)
    fig_grad = logit_mult * jnp.dot(
        coef_rows, all_cap.astype(jnp.float32), precision=lax.Precision.HIGHEST
    )
    cap_grad = logit_mult * jnp.dot(
        coef_cols, all_fig.astype(jnp.float32), precision=lax.Precision.HIGHEST
    )
    figure_direction = fig_inv * (
        fig_grad - fig_unit * jnp.sum(fig_unit * fig_grad, axis=1, keepdims=True)
    )
    caption_direction = cap_inv * (
        cap_grad - cap_unit * jnp.sum(cap_unit * cap_grad, axis=1, keepdims=True)
    )
    slot_ct = (
        jnp.zeros((row_count, feature_width), jnp.float32)
        .at[fig_slot]
        .add(figure_direction)
        .at[cap_slot]
        .add(caption_direction)
    )
    branch_ct = pullback(slot_ct)[0]
    slot_gradient = (slot_ct + branch_ct.astype(jnp.float32)).astype(jnp.bfloat16)
    back_rows = select_rows_t(recv_onehot, slot_gradient)
    home_rows = lax.all_to_all(
        back_rows.reshape(dp_count, capacity, feature_width),
        "dp",
        split_axis=0,
        concat_axis=0,
        tiled=True,
    )
    page_grad = select_rows_t(send_onehot, home_rows.reshape(-1, feature_width))
    return (page_grad, pair_loss)


def solution(mesh):
    return jax.shard_map(
        body,
        mesh=mesh,
        in_specs=(
            P(("dp", "fsdp"), None),
            P(("dp", "fsdp")),
            P(("dp", "fsdp"), None),
            P(None, "fsdp", None),
            P(None, "fsdp"),
            P(("dp", "fsdp")),
            P(("dp", "fsdp")),
            P(),
            P(("dp", "fsdp")),
        ),
        out_specs=(P(("dp", "fsdp"), None), P(("dp", "fsdp"))),
        check_vma=False,
    )
```

```python
import math

import jax
import jax.numpy as jnp
from jax import lax
from jax.sharding import PartitionSpec as P

HD = 64


EPSILON = 1e-06


def log_total(values, axis):
    return jnp.log(jnp.sum(jnp.exp(values), axis=axis))


def attend(query_rows, slot_row_block, qkv_mat, out_mat, query_doc, doc_row):
    query_count = query_rows.shape[0]
    row_count = slot_row_block.shape[0]
    query_h = (
        jnp.dot(query_rows, qkv_mat[0], preferred_element_type=jnp.float32)
        .astype(jnp.bfloat16)
        .reshape(query_count, -1, HD)
    )
    key_h = (
        jnp.dot(slot_row_block, qkv_mat[1], preferred_element_type=jnp.float32)
        .astype(jnp.bfloat16)
        .reshape(row_count, -1, HD)
    )
    value_h = (
        jnp.dot(slot_row_block, qkv_mat[2], preferred_element_type=jnp.float32)
        .astype(jnp.bfloat16)
        .reshape(row_count, -1, HD)
    )
    scores = jnp.einsum("qhd,khd->hqk", query_h, key_h, preferred_element_type=jnp.float32) * (
        1.0 / math.sqrt(HD)
    )
    same_doc = query_doc[:, None] == doc_row[None, :]
    scores = jnp.where(same_doc[None], scores, -1e30)
    weights = jnp.exp(scores)
    attn_prob = (weights / jnp.sum(weights, axis=2, keepdims=True)).astype(jnp.bfloat16)
    mixed = jnp.einsum("hqk,khd->qhd", attn_prob, value_h, preferred_element_type=jnp.float32)
    mixed = mixed.astype(jnp.bfloat16).reshape(query_count, -1)
    return jnp.dot(mixed, out_mat, preferred_element_type=jnp.float32)


def select_rows(onehot, rows):
    picked = jnp.dot(onehot, rows, preferred_element_type=jnp.float32)
    return picked.astype(rows.dtype)


def select_rows_t(onehot, rows):
    picked = lax.dot_general(
        onehot, rows, (((0,), (0,)), ((), ())), preferred_element_type=jnp.float32
    )
    return picked.astype(rows.dtype)


def body(
    page_embed,
    page_slot,
    doc_ids,
    qkv_weight,
    out_weight,
    fig_slot,
    cap_slot,
    logit_scale,
    loss_cotangent,
):
    dp_count = lax.axis_size("dp")
    row_count = page_embed.shape[0]
    feature_width = page_embed.shape[1]
    capacity = 5 * row_count // (4 * dp_count)
    buffer_rows = dp_count * capacity
    owner_idx = page_slot // row_count
    slot_idx = page_slot % row_count
    onehot = (owner_idx[:, None] == jnp.arange(dp_count)[None, :]).astype(jnp.int32)
    rank_idx = jnp.sum((jnp.cumsum(onehot, axis=0) - onehot) * onehot, axis=1)
    dest = owner_idx * capacity + rank_idx
    send_match = dest[None, :] == jnp.arange(buffer_rows)[:, None]
    send_onehot = send_match.astype(jnp.bfloat16)
    send_rows = select_rows(send_onehot, page_embed)
    send_ids = jnp.where(
        jnp.any(send_match, axis=1),
        jnp.sum(jnp.where(send_match, slot_idx[None, :], 0), axis=1),
        row_count,
    ).reshape(dp_count, capacity)
    recv_rows, recv_ids = (
        lax.all_to_all(
            send_rows.reshape(dp_count, capacity, feature_width),
            "dp",
            split_axis=0,
            concat_axis=0,
            tiled=True,
        ),
        lax.all_to_all(send_ids, "dp", split_axis=0, concat_axis=0, tiled=True),
    )
    flat_ids = recv_ids.reshape(-1)
    recv_onehot = (jnp.arange(row_count)[:, None] == flat_ids[None, :]).astype(jnp.bfloat16)
    slot_row_block = select_rows(recv_onehot, recv_rows.reshape(-1, feature_width))
    qkv_full, out_full = (
        lax.all_gather(qkv_weight, "fsdp", axis=1, tiled=True),
        lax.all_gather(out_weight, "fsdp", axis=1, tiled=True),
    )
    doc_row = doc_ids[0]
    pair_count = fig_slot.shape[0]
    query_slots = jnp.concatenate([fig_slot, cap_slot], axis=0)
    query_onehot = (query_slots[:, None] == jnp.arange(row_count)[None, :]).astype(jnp.bfloat16)
    query_doc = jnp.sum(
        jnp.where(query_slots[:, None] == jnp.arange(row_count)[None, :], doc_row[None, :], 0),
        axis=1,
    )

    def branch(inputs):
        picked = select_rows(query_onehot, inputs)
        return attend(picked, inputs, qkv_full, out_full, query_doc, doc_row)

    attn_out, pullback = jax.vjp(branch, slot_row_block)
    query_rows = select_rows(query_onehot, slot_row_block)
    query_output = query_rows.astype(jnp.float32) + attn_out
    fig_vec = query_output[:pair_count]
    cap_vec = query_output[pair_count:]
    fig_inv = lax.rsqrt(jnp.sum(fig_vec * fig_vec, axis=1, keepdims=True) + EPSILON)
    cap_inv = lax.rsqrt(jnp.sum(cap_vec * cap_vec, axis=1, keepdims=True) + EPSILON)
    fig_unit = fig_vec * fig_inv
    cap_unit = cap_vec * cap_inv
    fig_emb = fig_unit.astype(jnp.bfloat16)
    cap_emb = cap_unit.astype(jnp.bfloat16)
    weight_hi = loss_cotangent.astype(jnp.bfloat16)
    weight_lo = (loss_cotangent - weight_hi.astype(jnp.float32)).astype(jnp.bfloat16)
    weight_rows = jnp.zeros((2, feature_width), jnp.bfloat16)
    weight_rows = weight_rows.at[0, :pair_count].set(weight_hi).at[1, :pair_count].set(weight_lo)
    both_emb = jnp.concatenate([fig_emb, cap_emb, weight_rows], axis=0)
    all_both = lax.all_gather(both_emb, "dp", axis=0, tiled=False)
    all_fig = all_both[:, :pair_count].reshape(-1, feature_width)
    all_cap = all_both[:, pair_count : 2 * pair_count].reshape(-1, feature_width)
    all_weight = (
        all_both[:, 2 * pair_count, :pair_count].astype(jnp.float32)
        + all_both[:, 2 * pair_count + 1, :pair_count].astype(jnp.float32)
    ).reshape(-1)
    logit_mult = logit_scale[0]
    pair_total = all_fig.shape[0]
    first_pair = lax.axis_index("dp") * pair_count
    logits = logit_mult * jnp.dot(all_fig, all_cap.T, preferred_element_type=jnp.float32)
    row_lse = log_total(logits, 1)
    col_lse = log_total(logits, 0)
    eye_mat = jnp.eye(pair_total, dtype=jnp.float32)
    diag_logit = jnp.sum(logits * eye_mat, axis=1)
    own_rows = first_pair + jnp.arange(pair_count)
    own_mask = (jnp.arange(pair_total)[None, :] == own_rows[:, None]).astype(jnp.float32)
    loss_all = 0.5 * (row_lse - diag_logit) + 0.5 * (col_lse - diag_logit)
    pair_loss = jnp.dot(own_mask, loss_all, precision=lax.Precision.HIGHEST)
    prob_rows = jnp.exp(logits - row_lse[:, None])
    prob_cols = jnp.exp(logits - col_lse[None, :])
    coef = 0.5 * all_weight[:, None] * (prob_rows - eye_mat) + 0.5 * (
        prob_cols - eye_mat
    ) * all_weight[None, :]
    coef_rows = jnp.dot(own_mask, coef, precision=lax.Precision.HIGHEST)
    coef_cols = jnp.dot(own_mask, coef.T, precision=lax.Precision.HIGHEST)
    fig_grad = logit_mult * jnp.dot(
        coef_rows, all_cap.astype(jnp.float32), precision=lax.Precision.HIGHEST
    )
    cap_grad = logit_mult * jnp.dot(
        coef_cols, all_fig.astype(jnp.float32), precision=lax.Precision.HIGHEST
    )
    figure_direction = fig_inv * (
        fig_grad - fig_unit * jnp.sum(fig_unit * fig_grad, axis=1, keepdims=True)
    )
    caption_direction = cap_inv * (
        cap_grad - cap_unit * jnp.sum(cap_unit * cap_grad, axis=1, keepdims=True)
    )
    query_ct = jnp.concatenate([figure_direction, caption_direction], axis=0)
    slot_ct = lax.dot_general(
        query_onehot.astype(jnp.float32),
        query_ct,
        (((0,), (0,)), ((), ())),
        precision=lax.Precision.HIGHEST,
    )
    branch_ct = pullback(query_ct)[0]
    slot_gradient = (slot_ct + branch_ct.astype(jnp.float32)).astype(jnp.bfloat16)
    back_rows = select_rows_t(recv_onehot, slot_gradient)
    home_rows = lax.all_to_all(
        back_rows.reshape(dp_count, capacity, feature_width),
        "dp",
        split_axis=0,
        concat_axis=0,
        tiled=True,
    )
    page_grad = select_rows_t(send_onehot, home_rows.reshape(-1, feature_width))
    return (page_grad, pair_loss)


def solution(mesh):
    return jax.shard_map(
        body,
        mesh=mesh,
        in_specs=(
            P(("dp", "fsdp"), None),
            P(("dp", "fsdp")),
            P(("dp", "fsdp"), None),
            P(None, "fsdp", None),
            P(None, "fsdp"),
            P(("dp", "fsdp")),
            P(("dp", "fsdp")),
            P(),
            P(("dp", "fsdp")),
        ),
        out_specs=(P(("dp", "fsdp"), None), P(("dp", "fsdp"))),
        check_vma=False,
    )
```

```python
import math

import jax
import jax.numpy as jnp
from jax import lax
from jax.sharding import PartitionSpec as P

HD = 64


EPSILON = 1e-06


def log_total(values, axis):
    return jnp.log(jnp.sum(jnp.exp(values), axis=axis))


def attend(query_rows, slot_row_block, qkv_mat, out_mat, query_doc, doc_row):
    query_count = query_rows.shape[0]
    row_count = slot_row_block.shape[0]
    query_h = (
        jnp.dot(query_rows, qkv_mat[0], preferred_element_type=jnp.float32)
        .astype(jnp.bfloat16)
        .reshape(query_count, -1, HD)
    )
    key_h = (
        jnp.dot(slot_row_block, qkv_mat[1], preferred_element_type=jnp.float32)
        .astype(jnp.bfloat16)
        .reshape(row_count, -1, HD)
    )
    value_h = (
        jnp.dot(slot_row_block, qkv_mat[2], preferred_element_type=jnp.float32)
        .astype(jnp.bfloat16)
        .reshape(row_count, -1, HD)
    )
    scores = jnp.einsum("qhd,khd->hqk", query_h, key_h, preferred_element_type=jnp.float32) * (
        1.0 / math.sqrt(HD)
    )
    same_doc = query_doc[:, None] == doc_row[None, :]
    scores = jnp.where(same_doc[None], scores, -1e30)
    weights = jnp.exp(scores)
    attn_prob = (weights / jnp.sum(weights, axis=2, keepdims=True)).astype(jnp.bfloat16)
    mixed = jnp.einsum("hqk,khd->qhd", attn_prob, value_h, preferred_element_type=jnp.float32)
    mixed = mixed.astype(jnp.bfloat16).reshape(query_count, -1)
    return jnp.dot(mixed, out_mat, preferred_element_type=jnp.float32)


def select_rows(onehot, rows):
    picked = jnp.dot(onehot, rows, preferred_element_type=jnp.float32)
    return picked.astype(rows.dtype)


def select_rows_t(onehot, rows):
    picked = lax.dot_general(
        onehot, rows, (((0,), (0,)), ((), ())), preferred_element_type=jnp.float32
    )
    return picked.astype(rows.dtype)


def body(
    page_embed,
    page_slot,
    doc_ids,
    qkv_weight,
    out_weight,
    fig_slot,
    cap_slot,
    logit_scale,
    loss_cotangent,
):
    dp_count = lax.axis_size("dp")
    row_count = page_embed.shape[0]
    feature_width = page_embed.shape[1]
    capacity = 5 * row_count // (4 * dp_count)
    buffer_rows = dp_count * capacity
    owner_idx = page_slot // row_count
    slot_idx = page_slot % row_count
    onehot = (owner_idx[:, None] == jnp.arange(dp_count)[None, :]).astype(jnp.int32)
    rank_idx = jnp.sum((jnp.cumsum(onehot, axis=0) - onehot) * onehot, axis=1)
    dest = owner_idx * capacity + rank_idx
    send_match = dest[None, :] == jnp.arange(buffer_rows)[:, None]
    send_onehot = send_match.astype(jnp.bfloat16).reshape(dp_count, capacity, row_count)
    send_rows = jnp.einsum(
        "opk,kd->opd", send_onehot, page_embed, preferred_element_type=jnp.float32
    ).astype(jnp.bfloat16)
    send_ids = jnp.where(
        jnp.any(send_match, axis=1),
        jnp.sum(jnp.where(send_match, slot_idx[None, :], 0), axis=1),
        row_count,
    ).reshape(dp_count, capacity)
    recv_rows, recv_ids = (
        lax.all_to_all(
            send_rows,
            "dp",
            split_axis=0,
            concat_axis=0,
            tiled=True,
        ),
        lax.all_to_all(send_ids, "dp", split_axis=0, concat_axis=0, tiled=True),
    )
    recv_onehot = (
        jnp.arange(row_count)[:, None, None] == recv_ids[None, :, :]
    ).astype(jnp.bfloat16)
    slot_row_block = jnp.einsum(
        "sop,opd->sd", recv_onehot, recv_rows, preferred_element_type=jnp.float32
    ).astype(jnp.bfloat16)
    qkv_full, out_full = (
        lax.all_gather(qkv_weight, "fsdp", axis=1, tiled=True),
        lax.all_gather(out_weight, "fsdp", axis=1, tiled=True),
    )
    doc_row = doc_ids[0]
    pair_count = fig_slot.shape[0]
    query_slots = jnp.concatenate([fig_slot, cap_slot], axis=0)
    query_onehot = (query_slots[:, None] == jnp.arange(row_count)[None, :]).astype(jnp.bfloat16)
    query_doc = jnp.sum(
        jnp.where(query_slots[:, None] == jnp.arange(row_count)[None, :], doc_row[None, :], 0),
        axis=1,
    )

    def branch(inputs):
        picked = select_rows(query_onehot, inputs)
        return attend(picked, inputs, qkv_full, out_full, query_doc, doc_row)

    attn_out, pullback = jax.vjp(branch, slot_row_block)
    query_rows = select_rows(query_onehot, slot_row_block)
    query_output = query_rows.astype(jnp.float32) + attn_out
    fig_vec = query_output[:pair_count]
    cap_vec = query_output[pair_count:]
    fig_inv = lax.rsqrt(jnp.sum(fig_vec * fig_vec, axis=1, keepdims=True) + EPSILON)
    cap_inv = lax.rsqrt(jnp.sum(cap_vec * cap_vec, axis=1, keepdims=True) + EPSILON)
    fig_unit = fig_vec * fig_inv
    cap_unit = cap_vec * cap_inv
    fig_emb = fig_unit.astype(jnp.bfloat16)
    cap_emb = cap_unit.astype(jnp.bfloat16)
    weight_hi = loss_cotangent.astype(jnp.bfloat16)
    weight_lo = (loss_cotangent - weight_hi.astype(jnp.float32)).astype(jnp.bfloat16)
    weight_rows = jnp.zeros((2, feature_width), jnp.bfloat16)
    weight_rows = weight_rows.at[0, :pair_count].set(weight_hi).at[1, :pair_count].set(weight_lo)
    both_emb = jnp.concatenate([fig_emb, cap_emb, weight_rows], axis=0)
    gathered = [both_emb]
    for shift in range(1, dp_count):
        gathered.append(
            lax.ppermute(
                both_emb, "dp", perm=[(i, (i - shift) % dp_count) for i in range(dp_count)]
            )
        )
    all_both = jnp.stack(gathered, axis=0)
    all_fig = all_both[:, :pair_count].reshape(-1, feature_width)
    all_cap = all_both[:, pair_count : 2 * pair_count].reshape(-1, feature_width)
    all_weight = (
        all_both[:, 2 * pair_count, :pair_count].astype(jnp.float32)
        + all_both[:, 2 * pair_count + 1, :pair_count].astype(jnp.float32)
    ).reshape(-1)
    logit_mult = logit_scale[0]
    pair_total = all_fig.shape[0]
    first_pair = 0
    logits = logit_mult * jnp.dot(all_fig, all_cap.T, preferred_element_type=jnp.float32)
    row_lse = log_total(logits, 1)
    col_lse = log_total(logits, 0)
    eye_mat = jnp.eye(pair_total, dtype=jnp.float32)
    diag_logit = jnp.sum(logits * eye_mat, axis=1)
    own_rows = first_pair + jnp.arange(pair_count)
    own_mask = (jnp.arange(pair_total)[None, :] == own_rows[:, None]).astype(jnp.float32)
    loss_all = 0.5 * (row_lse - diag_logit) + 0.5 * (col_lse - diag_logit)
    pair_loss = jnp.dot(own_mask, loss_all, precision=lax.Precision.HIGHEST)
    prob_rows = jnp.exp(logits - row_lse[:, None])
    prob_cols = jnp.exp(logits - col_lse[None, :])
    coef = 0.5 * all_weight[:, None] * (prob_rows - eye_mat) + 0.5 * (
        prob_cols - eye_mat
    ) * all_weight[None, :]
    coef_rows = jnp.dot(own_mask, coef, precision=lax.Precision.HIGHEST)
    coef_cols = jnp.dot(own_mask, coef.T, precision=lax.Precision.HIGHEST)
    fig_grad = logit_mult * jnp.dot(
        coef_rows, all_cap.astype(jnp.float32), precision=lax.Precision.HIGHEST
    )
    cap_grad = logit_mult * jnp.dot(
        coef_cols, all_fig.astype(jnp.float32), precision=lax.Precision.HIGHEST
    )
    figure_direction = fig_inv * (
        fig_grad - fig_unit * jnp.sum(fig_unit * fig_grad, axis=1, keepdims=True)
    )
    caption_direction = cap_inv * (
        cap_grad - cap_unit * jnp.sum(cap_unit * cap_grad, axis=1, keepdims=True)
    )
    query_ct = jnp.concatenate([figure_direction, caption_direction], axis=0)
    slot_ct = lax.dot_general(
        query_onehot.astype(jnp.float32),
        query_ct,
        (((0,), (0,)), ((), ())),
        precision=lax.Precision.HIGHEST,
    )
    branch_ct = pullback(query_ct)[0]
    slot_gradient = (slot_ct + branch_ct.astype(jnp.float32)).astype(jnp.bfloat16)
    back_rows = jnp.einsum(
        "sop,sd->opd", recv_onehot, slot_gradient, preferred_element_type=jnp.float32
    ).astype(jnp.bfloat16)
    home_rows = lax.all_to_all(back_rows, "dp", split_axis=0, concat_axis=0, tiled=True)
    page_grad = jnp.einsum(
        "opk,opd->kd", send_onehot, home_rows, preferred_element_type=jnp.float32
    ).astype(jnp.bfloat16)
    return (page_grad, pair_loss)


def solution(mesh):
    return jax.shard_map(
        body,
        mesh=mesh,
        in_specs=(
            P(("dp", "fsdp"), None),
            P(("dp", "fsdp")),
            P(("dp", "fsdp"), None),
            P(None, "fsdp", None),
            P(None, "fsdp"),
            P(("dp", "fsdp")),
            P(("dp", "fsdp")),
            P(),
            P(("dp", "fsdp")),
        ),
        out_specs=(P(("dp", "fsdp"), None), P(("dp", "fsdp"))),
        check_vma=False,
    )
```

```python
import math

import jax
import jax.numpy as jnp
from jax import lax
from jax.sharding import PartitionSpec as P

HD = 64


EPSILON = 1e-06


def log_total(values, axis):
    return jnp.log(jnp.sum(jnp.exp(values), axis=axis))


def attend(query_rows, slot_row_block, qkv_mat, out_mat, query_doc, doc_row):
    query_count = query_rows.shape[0]
    row_count = slot_row_block.shape[0]
    query_h = (
        jnp.dot(query_rows, qkv_mat[0], preferred_element_type=jnp.float32)
        .astype(jnp.bfloat16)
        .reshape(query_count, -1, HD)
    )
    key_h = (
        jnp.dot(slot_row_block, qkv_mat[1], preferred_element_type=jnp.float32)
        .astype(jnp.bfloat16)
        .reshape(row_count, -1, HD)
    )
    value_h = (
        jnp.dot(slot_row_block, qkv_mat[2], preferred_element_type=jnp.float32)
        .astype(jnp.bfloat16)
        .reshape(row_count, -1, HD)
    )
    scores = jnp.einsum("qhd,khd->hqk", query_h, key_h, preferred_element_type=jnp.float32) * (
        1.0 / math.sqrt(HD)
    )
    same_doc = query_doc[:, None] == doc_row[None, :]
    scores = jnp.where(same_doc[None], scores, -1e30)
    weights = jnp.exp(scores)
    attn_prob = (weights / jnp.sum(weights, axis=2, keepdims=True)).astype(jnp.bfloat16)
    mixed = jnp.einsum("hqk,khd->qhd", attn_prob, value_h, preferred_element_type=jnp.float32)
    mixed = mixed.astype(jnp.bfloat16).reshape(query_count, -1)
    return jnp.dot(mixed, out_mat, preferred_element_type=jnp.float32)


def select_rows(onehot, rows):
    picked = jnp.dot(onehot, rows, preferred_element_type=jnp.float32)
    return picked.astype(rows.dtype)


def select_rows_t(onehot, rows):
    picked = lax.dot_general(
        onehot, rows, (((0,), (0,)), ((), ())), preferred_element_type=jnp.float32
    )
    return picked.astype(rows.dtype)


def body(
    page_embed,
    page_slot,
    doc_ids,
    qkv_weight,
    out_weight,
    fig_slot,
    cap_slot,
    logit_scale,
    loss_cotangent,
):
    dp_count = lax.axis_size("dp")
    row_count = page_embed.shape[0]
    feature_width = page_embed.shape[1]
    capacity = 5 * row_count // (4 * dp_count)
    buffer_rows = dp_count * capacity
    owner_idx = page_slot // row_count
    slot_idx = page_slot % row_count
    onehot = (owner_idx[:, None] == jnp.arange(dp_count)[None, :]).astype(jnp.int32)
    rank_idx = jnp.sum((jnp.cumsum(onehot, axis=0) - onehot) * onehot, axis=1)
    dest = owner_idx * capacity + rank_idx
    send_match = dest[None, :] == jnp.arange(buffer_rows)[:, None]
    send_onehot = send_match.astype(jnp.bfloat16).reshape(dp_count, capacity, row_count)
    send_rows = jnp.einsum(
        "opk,kd->opd", send_onehot, page_embed, preferred_element_type=jnp.float32
    ).astype(jnp.bfloat16)
    send_ids = jnp.where(
        jnp.any(send_match, axis=1),
        jnp.sum(jnp.where(send_match, slot_idx[None, :], 0), axis=1),
        row_count,
    ).reshape(dp_count, capacity)
    recv_rows, recv_ids = (
        lax.all_to_all(
            send_rows,
            "dp",
            split_axis=0,
            concat_axis=0,
            tiled=True,
        ),
        lax.all_to_all(send_ids, "dp", split_axis=0, concat_axis=0, tiled=True),
    )
    recv_onehot = (
        jnp.arange(row_count)[:, None, None] == recv_ids[None, :, :]
    ).astype(jnp.bfloat16)
    slot_row_block = jnp.einsum(
        "sop,opd->sd", recv_onehot, recv_rows, preferred_element_type=jnp.float32
    ).astype(jnp.bfloat16)
    qkv_full, out_full = (
        lax.all_gather(qkv_weight, "fsdp", axis=1, tiled=True),
        lax.all_gather(out_weight, "fsdp", axis=1, tiled=True),
    )
    doc_row = doc_ids[0]
    pair_count = fig_slot.shape[0]
    query_slots = jnp.concatenate([fig_slot, cap_slot], axis=0)
    query_onehot = (query_slots[:, None] == jnp.arange(row_count)[None, :]).astype(jnp.bfloat16)
    query_doc = jnp.sum(
        jnp.where(query_slots[:, None] == jnp.arange(row_count)[None, :], doc_row[None, :], 0),
        axis=1,
    )

    def branch(inputs):
        picked = select_rows(query_onehot, inputs)
        return attend(picked, inputs, qkv_full, out_full, query_doc, doc_row)

    attn_out, pullback = jax.vjp(branch, slot_row_block)
    query_rows = select_rows(query_onehot, slot_row_block)
    query_output = query_rows.astype(jnp.float32) + attn_out
    fig_vec = query_output[:pair_count]
    cap_vec = query_output[pair_count:]
    fig_inv = lax.rsqrt(jnp.sum(fig_vec * fig_vec, axis=1, keepdims=True) + EPSILON)
    cap_inv = lax.rsqrt(jnp.sum(cap_vec * cap_vec, axis=1, keepdims=True) + EPSILON)
    fig_unit = fig_vec * fig_inv
    cap_unit = cap_vec * cap_inv
    fig_emb = fig_unit.astype(jnp.bfloat16)
    cap_emb = cap_unit.astype(jnp.bfloat16)
    weight_hi = loss_cotangent.astype(jnp.bfloat16)
    weight_lo = (loss_cotangent - weight_hi.astype(jnp.float32)).astype(jnp.bfloat16)
    weight_rows = jnp.zeros((2, feature_width), jnp.bfloat16)
    weight_rows = weight_rows.at[0, :pair_count].set(weight_hi).at[1, :pair_count].set(weight_lo)
    both_emb = jnp.concatenate([fig_emb, cap_emb, weight_rows], axis=0)
    all_both = lax.all_to_all(
        jnp.broadcast_to(both_emb[None], (dp_count,) + both_emb.shape),
        "dp",
        split_axis=0,
        concat_axis=0,
        tiled=True,
    )
    all_fig = all_both[:, :pair_count].reshape(-1, feature_width)
    all_cap = all_both[:, pair_count : 2 * pair_count].reshape(-1, feature_width)
    all_weight = (
        all_both[:, 2 * pair_count, :pair_count].astype(jnp.float32)
        + all_both[:, 2 * pair_count + 1, :pair_count].astype(jnp.float32)
    ).reshape(-1)
    logit_mult = logit_scale[0]
    pair_total = all_fig.shape[0]
    first_pair = lax.axis_index("dp") * pair_count
    logits = logit_mult * jnp.dot(all_fig, all_cap.T, preferred_element_type=jnp.float32)
    row_lse = log_total(logits, 1)
    col_lse = log_total(logits, 0)
    eye_mat = jnp.eye(pair_total, dtype=jnp.float32)
    diag_logit = jnp.sum(logits * eye_mat, axis=1)
    own_rows = first_pair + jnp.arange(pair_count)
    own_mask = (jnp.arange(pair_total)[None, :] == own_rows[:, None]).astype(jnp.float32)
    loss_all = 0.5 * (row_lse - diag_logit) + 0.5 * (col_lse - diag_logit)
    pair_loss = jnp.dot(own_mask, loss_all, precision=lax.Precision.HIGHEST)
    prob_rows = jnp.exp(logits - row_lse[:, None])
    prob_cols = jnp.exp(logits - col_lse[None, :])
    coef = 0.5 * all_weight[:, None] * (prob_rows - eye_mat) + 0.5 * (
        prob_cols - eye_mat
    ) * all_weight[None, :]
    coef_rows = jnp.dot(own_mask, coef, precision=lax.Precision.HIGHEST)
    coef_cols = jnp.dot(own_mask, coef.T, precision=lax.Precision.HIGHEST)
    fig_grad = logit_mult * jnp.dot(
        coef_rows, all_cap.astype(jnp.float32), precision=lax.Precision.HIGHEST
    )
    cap_grad = logit_mult * jnp.dot(
        coef_cols, all_fig.astype(jnp.float32), precision=lax.Precision.HIGHEST
    )
    figure_direction = fig_inv * (
        fig_grad - fig_unit * jnp.sum(fig_unit * fig_grad, axis=1, keepdims=True)
    )
    caption_direction = cap_inv * (
        cap_grad - cap_unit * jnp.sum(cap_unit * cap_grad, axis=1, keepdims=True)
    )
    query_ct = jnp.concatenate([figure_direction, caption_direction], axis=0)
    slot_ct = lax.dot_general(
        query_onehot.astype(jnp.float32),
        query_ct,
        (((0,), (0,)), ((), ())),
        precision=lax.Precision.HIGHEST,
    )
    branch_ct = pullback(query_ct)[0]
    slot_gradient = (slot_ct + branch_ct.astype(jnp.float32)).astype(jnp.bfloat16)
    back_rows = jnp.einsum(
        "sop,sd->opd", recv_onehot, slot_gradient, preferred_element_type=jnp.float32
    ).astype(jnp.bfloat16)
    home_rows = lax.all_to_all(back_rows, "dp", split_axis=0, concat_axis=0, tiled=True)
    page_grad = jnp.einsum(
        "opk,opd->kd", send_onehot, home_rows, preferred_element_type=jnp.float32
    ).astype(jnp.bfloat16)
    return (page_grad, pair_loss)


def solution(mesh):
    return jax.shard_map(
        body,
        mesh=mesh,
        in_specs=(
            P(("dp", "fsdp"), None),
            P(("dp", "fsdp")),
            P(("dp", "fsdp"), None),
            P(None, "fsdp", None),
            P(None, "fsdp"),
            P(("dp", "fsdp")),
            P(("dp", "fsdp")),
            P(),
            P(("dp", "fsdp")),
        ),
        out_specs=(P(("dp", "fsdp"), None), P(("dp", "fsdp"))),
        check_vma=False,
    )
```

```python
import math

import jax
import jax.numpy as jnp
from jax import lax
from jax.sharding import PartitionSpec as P

HD = 64


EPSILON = 1e-06


def log_total(values, axis):
    return jnp.log(jnp.sum(jnp.exp(values), axis=axis))


def attend(query_rows, slot_row_block, qkv_mat, out_mat, query_doc, doc_row):
    query_count = query_rows.shape[0]
    row_count = slot_row_block.shape[0]
    query_h = (
        jnp.dot(query_rows, qkv_mat[0], preferred_element_type=jnp.float32)
        .astype(jnp.bfloat16)
        .reshape(query_count, -1, HD)
    )
    key_h = (
        jnp.dot(slot_row_block, qkv_mat[1], preferred_element_type=jnp.float32)
        .astype(jnp.bfloat16)
        .reshape(row_count, -1, HD)
    )
    value_h = (
        jnp.dot(slot_row_block, qkv_mat[2], preferred_element_type=jnp.float32)
        .astype(jnp.bfloat16)
        .reshape(row_count, -1, HD)
    )
    scores = jnp.einsum("qhd,khd->hqk", query_h, key_h, preferred_element_type=jnp.float32) * (
        1.0 / math.sqrt(HD)
    )
    same_doc = query_doc[:, None] == doc_row[None, :]
    scores = jnp.where(same_doc[None], scores, -1e30)
    weights = jnp.exp(scores)
    attn_prob = (weights / jnp.sum(weights, axis=2, keepdims=True)).astype(jnp.bfloat16)
    mixed = jnp.einsum("hqk,khd->qhd", attn_prob, value_h, preferred_element_type=jnp.float32)
    mixed = mixed.astype(jnp.bfloat16).reshape(query_count, -1)
    return jnp.dot(mixed, out_mat, preferred_element_type=jnp.float32)


def select_rows(onehot, rows):
    picked = jnp.dot(onehot, rows, preferred_element_type=jnp.float32)
    return picked.astype(rows.dtype)


def select_rows_t(onehot, rows):
    picked = lax.dot_general(
        onehot, rows, (((0,), (0,)), ((), ())), preferred_element_type=jnp.float32
    )
    return picked.astype(rows.dtype)


def body(
    page_embed,
    page_slot,
    doc_ids,
    qkv_weight,
    out_weight,
    fig_slot,
    cap_slot,
    logit_scale,
    loss_cotangent,
):
    dp_count = lax.axis_size("dp")
    row_count = page_embed.shape[0]
    feature_width = page_embed.shape[1]
    capacity = 5 * row_count // (4 * dp_count)
    buffer_rows = dp_count * capacity
    owner_idx = page_slot // row_count
    slot_idx = page_slot % row_count
    onehot = (owner_idx[:, None] == jnp.arange(dp_count)[None, :]).astype(jnp.int32)
    rank_idx = jnp.sum((jnp.cumsum(onehot, axis=0) - onehot) * onehot, axis=1)
    dest = owner_idx * capacity + rank_idx
    send_match = dest[None, :] == jnp.arange(buffer_rows)[:, None]
    send_ids = jnp.where(
        jnp.any(send_match, axis=1),
        jnp.sum(jnp.where(send_match, slot_idx[None, :], 0), axis=1),
        row_count,
    ).reshape(dp_count, capacity)
    send_onehot = jnp.concatenate(
        [
            send_match.astype(jnp.bfloat16).reshape(dp_count, capacity, row_count),
            jnp.zeros((dp_count, 1, row_count), jnp.bfloat16),
        ],
        axis=1,
    )
    id_lanes = jnp.zeros((dp_count, feature_width), jnp.float32)
    id_lanes = id_lanes.at[:, :capacity].set((send_ids // 16).astype(jnp.float32))
    id_lanes = id_lanes.at[:, 128 : 128 + capacity].set((send_ids % 16).astype(jnp.float32))
    id_rows = jnp.concatenate(
        [jnp.zeros((dp_count, capacity, feature_width), jnp.float32), id_lanes[:, None, :]], axis=1
    )
    send_rows = (
        jnp.einsum("opk,kd->opd", send_onehot, page_embed, preferred_element_type=jnp.float32)
        + id_rows
    ).astype(jnp.bfloat16)
    recv_rows = lax.all_to_all(send_rows, "dp", split_axis=0, concat_axis=0, tiled=True)
    id_row = recv_rows[:, capacity, :].astype(jnp.float32)
    recv_ids = (
        id_row[:, :capacity].astype(jnp.int32) * 16
        + id_row[:, 128 : 128 + capacity].astype(jnp.int32)
    )
    recv_ids = jnp.concatenate([recv_ids, jnp.full((dp_count, 1), row_count, jnp.int32)], axis=1)
    recv_onehot = (
        jnp.arange(row_count)[:, None, None] == recv_ids[None, :, :]
    ).astype(jnp.bfloat16)
    slot_row_block = jnp.einsum(
        "sop,opd->sd", recv_onehot, recv_rows, preferred_element_type=jnp.float32
    ).astype(jnp.bfloat16)
    qkv_full, out_full = (
        lax.all_gather(qkv_weight, "fsdp", axis=1, tiled=True),
        lax.all_gather(out_weight, "fsdp", axis=1, tiled=True),
    )
    doc_row = doc_ids[0]
    pair_count = fig_slot.shape[0]
    query_slots = jnp.concatenate([fig_slot, cap_slot], axis=0)
    query_onehot = (query_slots[:, None] == jnp.arange(row_count)[None, :]).astype(jnp.bfloat16)
    query_doc = jnp.sum(
        jnp.where(query_slots[:, None] == jnp.arange(row_count)[None, :], doc_row[None, :], 0),
        axis=1,
    )

    def branch(inputs):
        picked = select_rows(query_onehot, inputs)
        return attend(picked, inputs, qkv_full, out_full, query_doc, doc_row)

    attn_out, pullback = jax.vjp(branch, slot_row_block)
    query_rows = select_rows(query_onehot, slot_row_block)
    query_output = query_rows.astype(jnp.float32) + attn_out
    fig_vec = query_output[:pair_count]
    cap_vec = query_output[pair_count:]
    fig_inv = lax.rsqrt(jnp.sum(fig_vec * fig_vec, axis=1, keepdims=True) + EPSILON)
    cap_inv = lax.rsqrt(jnp.sum(cap_vec * cap_vec, axis=1, keepdims=True) + EPSILON)
    fig_unit = fig_vec * fig_inv
    cap_unit = cap_vec * cap_inv
    fig_emb = fig_unit.astype(jnp.bfloat16)
    cap_emb = cap_unit.astype(jnp.bfloat16)
    weight_hi = loss_cotangent.astype(jnp.bfloat16)
    weight_lo = (loss_cotangent - weight_hi.astype(jnp.float32)).astype(jnp.bfloat16)
    weight_rows = jnp.zeros((2, feature_width), jnp.bfloat16)
    weight_rows = weight_rows.at[0, :pair_count].set(weight_hi).at[1, :pair_count].set(weight_lo)
    both_emb = jnp.concatenate([fig_emb, cap_emb, weight_rows], axis=0)
    all_both = lax.all_to_all(
        jnp.broadcast_to(both_emb[None], (dp_count,) + both_emb.shape),
        "dp",
        split_axis=0,
        concat_axis=0,
        tiled=True,
    )
    all_fig = all_both[:, :pair_count].reshape(-1, feature_width)
    all_cap = all_both[:, pair_count : 2 * pair_count].reshape(-1, feature_width)
    all_weight = (
        all_both[:, 2 * pair_count, :pair_count].astype(jnp.float32)
        + all_both[:, 2 * pair_count + 1, :pair_count].astype(jnp.float32)
    ).reshape(-1)
    logit_mult = logit_scale[0]
    pair_total = all_fig.shape[0]
    first_pair = lax.axis_index("dp") * pair_count
    logits = logit_mult * jnp.dot(all_fig, all_cap.T, preferred_element_type=jnp.float32)
    row_lse = log_total(logits, 1)
    col_lse = log_total(logits, 0)
    eye_mat = jnp.eye(pair_total, dtype=jnp.float32)
    diag_logit = jnp.sum(logits * eye_mat, axis=1)
    own_rows = first_pair + jnp.arange(pair_count)
    own_mask = (jnp.arange(pair_total)[None, :] == own_rows[:, None]).astype(jnp.float32)
    loss_all = 0.5 * (row_lse - diag_logit) + 0.5 * (col_lse - diag_logit)
    pair_loss = jnp.dot(own_mask, loss_all, precision=lax.Precision.HIGHEST)
    prob_rows = jnp.exp(logits - row_lse[:, None])
    prob_cols = jnp.exp(logits - col_lse[None, :])
    coef = 0.5 * all_weight[:, None] * (prob_rows - eye_mat) + 0.5 * (
        prob_cols - eye_mat
    ) * all_weight[None, :]
    coef_rows = jnp.dot(own_mask, coef, precision=lax.Precision.HIGHEST)
    coef_cols = jnp.dot(own_mask, coef.T, precision=lax.Precision.HIGHEST)
    fig_grad = logit_mult * jnp.dot(
        coef_rows, all_cap.astype(jnp.float32), precision=lax.Precision.HIGHEST
    )
    cap_grad = logit_mult * jnp.dot(
        coef_cols, all_fig.astype(jnp.float32), precision=lax.Precision.HIGHEST
    )
    figure_direction = fig_inv * (
        fig_grad - fig_unit * jnp.sum(fig_unit * fig_grad, axis=1, keepdims=True)
    )
    caption_direction = cap_inv * (
        cap_grad - cap_unit * jnp.sum(cap_unit * cap_grad, axis=1, keepdims=True)
    )
    query_ct = jnp.concatenate([figure_direction, caption_direction], axis=0)
    slot_ct = lax.dot_general(
        query_onehot.astype(jnp.float32),
        query_ct,
        (((0,), (0,)), ((), ())),
        precision=lax.Precision.HIGHEST,
    )
    branch_ct = pullback(query_ct)[0]
    slot_gradient = (slot_ct + branch_ct.astype(jnp.float32)).astype(jnp.bfloat16)
    back_rows = jnp.einsum(
        "sop,sd->opd", recv_onehot, slot_gradient, preferred_element_type=jnp.float32
    ).astype(jnp.bfloat16)
    home_rows = lax.all_to_all(back_rows, "dp", split_axis=0, concat_axis=0, tiled=True)
    page_grad = jnp.einsum(
        "opk,opd->kd", send_onehot, home_rows, preferred_element_type=jnp.float32
    ).astype(jnp.bfloat16)
    return (page_grad, pair_loss)


def solution(mesh):
    return jax.shard_map(
        body,
        mesh=mesh,
        in_specs=(
            P(("dp", "fsdp"), None),
            P(("dp", "fsdp")),
            P(("dp", "fsdp"), None),
            P(None, "fsdp", None),
            P(None, "fsdp"),
            P(("dp", "fsdp")),
            P(("dp", "fsdp")),
            P(),
            P(("dp", "fsdp")),
        ),
        out_specs=(P(("dp", "fsdp"), None), P(("dp", "fsdp"))),
        check_vma=False,
    )
```

```python
import math

import jax
import jax.numpy as jnp
from jax import lax
from jax.sharding import PartitionSpec as P

HD = 64


EPSILON = 1e-06


def log_total(values, axis):
    return jnp.log(jnp.sum(jnp.exp(values), axis=axis))


def attend(query_rows, slot_row_block, qkv_mat, out_mat, query_doc, doc_row, block_shift):
    query_count = query_rows.shape[0]
    row_count = slot_row_block.shape[0]
    query_h = (
        jnp.dot(query_rows, qkv_mat[0], preferred_element_type=jnp.float32)
        .astype(jnp.bfloat16)
        .reshape(query_count, -1, HD)
    )
    key_h = (
        jnp.dot(slot_row_block, qkv_mat[1], preferred_element_type=jnp.float32)
        .astype(jnp.bfloat16)
        .reshape(row_count, -1, HD)
    )
    value_h = (
        jnp.dot(slot_row_block, qkv_mat[2], preferred_element_type=jnp.float32)
        .astype(jnp.bfloat16)
        .reshape(row_count, -1, HD)
    )
    scores = jnp.einsum("qhd,khd->hqk", query_h, key_h, preferred_element_type=jnp.float32) * (
        1.0 / math.sqrt(HD)
    )
    same_doc = query_doc[:, None] == doc_row[None, :]
    scores = jnp.where(same_doc[None], scores, -1e30)
    weights = jnp.exp(scores)
    attn_prob = (weights / jnp.sum(weights, axis=2, keepdims=True)).astype(jnp.bfloat16)
    mixed = jnp.einsum("hqk,khd->qhd", attn_prob, value_h, preferred_element_type=jnp.float32)
    mixed = mixed.astype(jnp.bfloat16).reshape(query_count, -1)
    out_cols = jnp.einsum("qe,jec->qjc", mixed, out_mat, preferred_element_type=jnp.float32)
    return jnp.roll(out_cols, block_shift, axis=1).reshape(query_count, -1)


def select_rows(onehot, rows):
    picked = jnp.dot(onehot, rows, preferred_element_type=jnp.float32)
    return picked.astype(rows.dtype)


def select_rows_t(onehot, rows):
    picked = lax.dot_general(
        onehot, rows, (((0,), (0,)), ((), ())), preferred_element_type=jnp.float32
    )
    return picked.astype(rows.dtype)


def body(
    page_embed,
    page_slot,
    doc_ids,
    qkv_weight,
    out_weight,
    fig_slot,
    cap_slot,
    logit_scale,
    loss_cotangent,
):
    dp_count = lax.axis_size("dp")
    row_count = page_embed.shape[0]
    feature_width = page_embed.shape[1]
    capacity = 5 * row_count // (4 * dp_count)
    buffer_rows = dp_count * capacity
    owner_idx = page_slot // row_count
    slot_idx = page_slot % row_count
    onehot = (owner_idx[:, None] == jnp.arange(dp_count)[None, :]).astype(jnp.int32)
    rank_idx = jnp.sum((jnp.cumsum(onehot, axis=0) - onehot) * onehot, axis=1)
    dest = owner_idx * capacity + rank_idx
    send_match = dest[None, :] == jnp.arange(buffer_rows)[:, None]
    send_ids = jnp.where(
        jnp.any(send_match, axis=1),
        jnp.sum(jnp.where(send_match, slot_idx[None, :], 0), axis=1),
        row_count,
    ).reshape(dp_count, capacity)
    send_onehot = jnp.concatenate(
        [
            send_match.astype(jnp.bfloat16).reshape(dp_count, capacity, row_count),
            jnp.zeros((dp_count, 1, row_count), jnp.bfloat16),
        ],
        axis=1,
    )
    id_lanes = jnp.zeros((dp_count, feature_width), jnp.float32)
    id_lanes = id_lanes.at[:, :capacity].set((send_ids // 16).astype(jnp.float32))
    id_lanes = id_lanes.at[:, 128 : 128 + capacity].set((send_ids % 16).astype(jnp.float32))
    id_rows = jnp.concatenate(
        [jnp.zeros((dp_count, capacity, feature_width), jnp.float32), id_lanes[:, None, :]], axis=1
    )
    send_rows = (
        jnp.einsum("opk,kd->opd", send_onehot, page_embed, preferred_element_type=jnp.float32)
        + id_rows
    ).astype(jnp.bfloat16)
    recv_rows = lax.all_to_all(send_rows, "dp", split_axis=0, concat_axis=0, tiled=True)
    id_row = recv_rows[:, capacity, :].astype(jnp.float32)
    recv_ids = (
        id_row[:, :capacity].astype(jnp.int32) * 16
        + id_row[:, 128 : 128 + capacity].astype(jnp.int32)
    )
    recv_ids = jnp.concatenate([recv_ids, jnp.full((dp_count, 1), row_count, jnp.int32)], axis=1)
    recv_onehot = (
        jnp.arange(row_count)[:, None, None] == recv_ids[None, :, :]
    ).astype(jnp.bfloat16)
    slot_row_block = jnp.einsum(
        "sop,opd->sd", recv_onehot, recv_rows, preferred_element_type=jnp.float32
    ).astype(jnp.bfloat16)
    fsdp_count = lax.axis_size("fsdp")
    qkv_full = lax.all_gather(qkv_weight, "fsdp", axis=1, tiled=True)
    fsdp_index = lax.axis_index("fsdp")
    out_list = [out_weight]
    for shift in range(1, fsdp_count):
        out_list.append(
            lax.ppermute(
                out_weight, "fsdp", perm=[(i, (i - shift) % fsdp_count) for i in range(fsdp_count)]
            )
        )
    out_blocks = jnp.stack(out_list, axis=0)
    doc_row = doc_ids[0]
    pair_count = fig_slot.shape[0]
    query_slots = jnp.concatenate([fig_slot, cap_slot], axis=0)
    query_onehot = (query_slots[:, None] == jnp.arange(row_count)[None, :]).astype(jnp.bfloat16)
    query_doc = jnp.sum(
        jnp.where(query_slots[:, None] == jnp.arange(row_count)[None, :], doc_row[None, :], 0),
        axis=1,
    )

    def branch(inputs):
        picked = select_rows(query_onehot, inputs)
        return attend(picked, inputs, qkv_full, out_blocks, query_doc, doc_row, fsdp_index)

    attn_out, pullback = jax.vjp(branch, slot_row_block)
    query_rows = select_rows(query_onehot, slot_row_block)
    query_output = query_rows.astype(jnp.float32) + attn_out
    fig_vec = query_output[:pair_count]
    cap_vec = query_output[pair_count:]
    fig_inv = lax.rsqrt(jnp.sum(fig_vec * fig_vec, axis=1, keepdims=True) + EPSILON)
    cap_inv = lax.rsqrt(jnp.sum(cap_vec * cap_vec, axis=1, keepdims=True) + EPSILON)
    fig_unit = fig_vec * fig_inv
    cap_unit = cap_vec * cap_inv
    fig_emb = fig_unit.astype(jnp.bfloat16)
    cap_emb = cap_unit.astype(jnp.bfloat16)
    weight_hi = loss_cotangent.astype(jnp.bfloat16)
    weight_lo = (loss_cotangent - weight_hi.astype(jnp.float32)).astype(jnp.bfloat16)
    weight_rows = jnp.zeros((2, feature_width), jnp.bfloat16)
    weight_rows = weight_rows.at[0, :pair_count].set(weight_hi).at[1, :pair_count].set(weight_lo)
    both_emb = jnp.concatenate([fig_emb, cap_emb, weight_rows], axis=0)
    all_both = lax.all_to_all(
        jnp.broadcast_to(both_emb[None], (dp_count,) + both_emb.shape),
        "dp",
        split_axis=0,
        concat_axis=0,
        tiled=True,
    )
    all_fig = all_both[:, :pair_count].reshape(-1, feature_width)
    all_cap = all_both[:, pair_count : 2 * pair_count].reshape(-1, feature_width)
    all_weight = (
        all_both[:, 2 * pair_count, :pair_count].astype(jnp.float32)
        + all_both[:, 2 * pair_count + 1, :pair_count].astype(jnp.float32)
    ).reshape(-1)
    logit_mult = logit_scale[0]
    pair_total = all_fig.shape[0]
    first_pair = lax.axis_index("dp") * pair_count
    logits = logit_mult * jnp.dot(all_fig, all_cap.T, preferred_element_type=jnp.float32)
    row_lse = log_total(logits, 1)
    col_lse = log_total(logits, 0)
    eye_mat = jnp.eye(pair_total, dtype=jnp.float32)
    diag_logit = jnp.sum(logits * eye_mat, axis=1)
    own_rows = first_pair + jnp.arange(pair_count)
    own_mask = (jnp.arange(pair_total)[None, :] == own_rows[:, None]).astype(jnp.float32)
    loss_all = 0.5 * (row_lse - diag_logit) + 0.5 * (col_lse - diag_logit)
    pair_loss = jnp.dot(own_mask, loss_all, precision=lax.Precision.HIGHEST)
    prob_rows = jnp.exp(logits - row_lse[:, None])
    prob_cols = jnp.exp(logits - col_lse[None, :])
    coef = 0.5 * all_weight[:, None] * (prob_rows - eye_mat) + 0.5 * (
        prob_cols - eye_mat
    ) * all_weight[None, :]
    coef_rows = jnp.dot(own_mask, coef, precision=lax.Precision.HIGHEST)
    coef_cols = jnp.dot(own_mask, coef.T, precision=lax.Precision.HIGHEST)
    fig_grad = logit_mult * jnp.dot(
        coef_rows, all_cap.astype(jnp.float32), precision=lax.Precision.HIGHEST
    )
    cap_grad = logit_mult * jnp.dot(
        coef_cols, all_fig.astype(jnp.float32), precision=lax.Precision.HIGHEST
    )
    figure_direction = fig_inv * (
        fig_grad - fig_unit * jnp.sum(fig_unit * fig_grad, axis=1, keepdims=True)
    )
    caption_direction = cap_inv * (
        cap_grad - cap_unit * jnp.sum(cap_unit * cap_grad, axis=1, keepdims=True)
    )
    query_ct = jnp.concatenate([figure_direction, caption_direction], axis=0)
    slot_ct = lax.dot_general(
        query_onehot.astype(jnp.float32),
        query_ct,
        (((0,), (0,)), ((), ())),
        precision=lax.Precision.HIGHEST,
    )
    branch_ct = pullback(query_ct)[0]
    slot_gradient = (slot_ct + branch_ct.astype(jnp.float32)).astype(jnp.bfloat16)
    back_rows = jnp.einsum(
        "sop,sd->opd", recv_onehot, slot_gradient, preferred_element_type=jnp.float32
    ).astype(jnp.bfloat16)
    home_rows = lax.all_to_all(back_rows, "dp", split_axis=0, concat_axis=0, tiled=True)
    page_grad = jnp.einsum(
        "opk,opd->kd", send_onehot, home_rows, preferred_element_type=jnp.float32
    ).astype(jnp.bfloat16)
    return (page_grad, pair_loss)


def solution(mesh):
    return jax.shard_map(
        body,
        mesh=mesh,
        in_specs=(
            P(("dp", "fsdp"), None),
            P(("dp", "fsdp")),
            P(("dp", "fsdp"), None),
            P(None, "fsdp", None),
            P(None, "fsdp"),
            P(("dp", "fsdp")),
            P(("dp", "fsdp")),
            P(),
            P(("dp", "fsdp")),
        ),
        out_specs=(P(("dp", "fsdp"), None), P(("dp", "fsdp"))),
        check_vma=False,
    )
```

```python
import math

import jax
import jax.numpy as jnp
from jax import lax
from jax.sharding import PartitionSpec as P

HD = 64


EPSILON = 1e-06


def log_total(values, axis):
    return jnp.log(jnp.sum(jnp.exp(values), axis=axis))


def attend(query_rows, slot_row_block, qkv_mat, kv_mat, out_mat, query_doc, doc_row):
    query_count = query_rows.shape[0]
    row_count = slot_row_block.shape[0]
    query_h = (
        jnp.dot(query_rows, qkv_mat[0], preferred_element_type=jnp.float32)
        .astype(jnp.bfloat16)
        .reshape(query_count, -1, HD)
    )
    key_value = jnp.dot(slot_row_block, kv_mat, preferred_element_type=jnp.float32).astype(
        jnp.bfloat16
    )
    head_width = qkv_mat.shape[2]
    key_h = key_value[:, :head_width].reshape(row_count, -1, HD)
    value_h = key_value[:, head_width:].reshape(row_count, -1, HD)
    scores = jnp.einsum("qhd,khd->hqk", query_h, key_h, preferred_element_type=jnp.float32) * (
        1.0 / math.sqrt(HD)
    )
    same_doc = query_doc[:, None] == doc_row[None, :]
    scores = jnp.where(same_doc[None], scores, -1e30)
    weights = jnp.exp(scores)
    attn_prob = (weights / jnp.sum(weights, axis=2, keepdims=True)).astype(jnp.bfloat16)
    mixed = jnp.einsum("hqk,khd->qhd", attn_prob, value_h, preferred_element_type=jnp.float32)
    mixed = mixed.astype(jnp.bfloat16).reshape(query_count, -1)
    return jnp.dot(mixed, out_mat, preferred_element_type=jnp.float32)


def select_rows(onehot, rows):
    picked = jnp.dot(onehot, rows, preferred_element_type=jnp.float32)
    return picked.astype(rows.dtype)


def select_rows_t(onehot, rows):
    picked = lax.dot_general(
        onehot, rows, (((0,), (0,)), ((), ())), preferred_element_type=jnp.float32
    )
    return picked.astype(rows.dtype)


def body(
    page_embed,
    page_slot,
    doc_ids,
    qkv_weight,
    out_weight,
    fig_slot,
    cap_slot,
    logit_scale,
    loss_cotangent,
):
    dp_count = lax.axis_size("dp")
    row_count = page_embed.shape[0]
    feature_width = page_embed.shape[1]
    capacity = 5 * row_count // (4 * dp_count)
    buffer_rows = dp_count * capacity
    owner_idx = page_slot // row_count
    slot_idx = page_slot % row_count
    onehot = (owner_idx[:, None] == jnp.arange(dp_count)[None, :]).astype(jnp.int32)
    rank_idx = jnp.sum((jnp.cumsum(onehot, axis=0) - onehot) * onehot, axis=1)
    dest = owner_idx * capacity + rank_idx
    send_match = dest[None, :] == jnp.arange(buffer_rows)[:, None]
    send_ids = jnp.where(
        jnp.any(send_match, axis=1),
        jnp.sum(jnp.where(send_match, slot_idx[None, :], 0), axis=1),
        row_count,
    ).reshape(dp_count, capacity)
    send_onehot = jnp.concatenate(
        [
            send_match.astype(jnp.bfloat16).reshape(dp_count, capacity, row_count),
            jnp.zeros((dp_count, 1, row_count), jnp.bfloat16),
        ],
        axis=1,
    )
    id_lanes = jnp.zeros((dp_count, feature_width), jnp.float32)
    id_lanes = id_lanes.at[:, :capacity].set((send_ids // 16).astype(jnp.float32))
    id_lanes = id_lanes.at[:, 128 : 128 + capacity].set((send_ids % 16).astype(jnp.float32))
    id_rows = jnp.concatenate(
        [jnp.zeros((dp_count, capacity, feature_width), jnp.float32), id_lanes[:, None, :]], axis=1
    )
    send_rows = (
        jnp.einsum("opk,kd->opd", send_onehot, page_embed, preferred_element_type=jnp.float32)
        + id_rows
    ).astype(jnp.bfloat16)
    recv_rows = lax.all_to_all(send_rows, "dp", split_axis=0, concat_axis=0, tiled=True)
    id_row = recv_rows[:, capacity, :].astype(jnp.float32)
    recv_ids = (
        id_row[:, :capacity].astype(jnp.int32) * 16
        + id_row[:, 128 : 128 + capacity].astype(jnp.int32)
    )
    recv_ids = jnp.concatenate([recv_ids, jnp.full((dp_count, 1), row_count, jnp.int32)], axis=1)
    recv_onehot = (
        jnp.arange(row_count)[:, None, None] == recv_ids[None, :, :]
    ).astype(jnp.bfloat16)
    slot_row_block = jnp.einsum(
        "sop,opd->sd", recv_onehot, recv_rows, preferred_element_type=jnp.float32
    ).astype(jnp.bfloat16)
    qkv_full, out_full = (
        lax.all_gather(qkv_weight, "fsdp", axis=1, tiled=True),
        lax.all_gather(out_weight, "fsdp", axis=1, tiled=True),
    )
    kv_full = jnp.concatenate([qkv_full[1], qkv_full[2]], axis=1)
    doc_row = doc_ids[0]
    pair_count = fig_slot.shape[0]
    query_slots = jnp.concatenate([fig_slot, cap_slot], axis=0)
    query_onehot = (query_slots[:, None] == jnp.arange(row_count)[None, :]).astype(jnp.bfloat16)
    query_doc = jnp.sum(
        jnp.where(query_slots[:, None] == jnp.arange(row_count)[None, :], doc_row[None, :], 0),
        axis=1,
    )

    def branch(inputs):
        picked = select_rows(query_onehot, inputs)
        return attend(picked, inputs, qkv_full, kv_full, out_full, query_doc, doc_row)

    attn_out, pullback = jax.vjp(branch, slot_row_block)
    query_rows = select_rows(query_onehot, slot_row_block)
    query_output = query_rows.astype(jnp.float32) + attn_out
    fig_vec = query_output[:pair_count]
    cap_vec = query_output[pair_count:]
    fig_inv = lax.rsqrt(jnp.sum(fig_vec * fig_vec, axis=1, keepdims=True) + EPSILON)
    cap_inv = lax.rsqrt(jnp.sum(cap_vec * cap_vec, axis=1, keepdims=True) + EPSILON)
    fig_unit = fig_vec * fig_inv
    cap_unit = cap_vec * cap_inv
    fig_emb = fig_unit.astype(jnp.bfloat16)
    cap_emb = cap_unit.astype(jnp.bfloat16)
    weight_hi = loss_cotangent.astype(jnp.bfloat16)
    weight_lo = (loss_cotangent - weight_hi.astype(jnp.float32)).astype(jnp.bfloat16)
    weight_rows = jnp.zeros((2, feature_width), jnp.bfloat16)
    weight_rows = weight_rows.at[0, :pair_count].set(weight_hi).at[1, :pair_count].set(weight_lo)
    both_emb = jnp.concatenate([fig_emb, cap_emb, weight_rows], axis=0)
    all_both = lax.all_to_all(
        jnp.broadcast_to(both_emb[None], (dp_count,) + both_emb.shape),
        "dp",
        split_axis=0,
        concat_axis=0,
        tiled=True,
    )
    all_fig = all_both[:, :pair_count].reshape(-1, feature_width)
    all_cap = all_both[:, pair_count : 2 * pair_count].reshape(-1, feature_width)
    all_weight = (
        all_both[:, 2 * pair_count, :pair_count].astype(jnp.float32)
        + all_both[:, 2 * pair_count + 1, :pair_count].astype(jnp.float32)
    ).reshape(-1)
    logit_mult = logit_scale[0]
    pair_total = all_fig.shape[0]
    first_pair = lax.axis_index("dp") * pair_count
    logits = logit_mult * jnp.dot(all_fig, all_cap.T, preferred_element_type=jnp.float32)
    row_lse = log_total(logits, 1)
    col_lse = log_total(logits, 0)
    eye_mat = jnp.eye(pair_total, dtype=jnp.float32)
    diag_logit = jnp.sum(logits * eye_mat, axis=1)
    own_rows = first_pair + jnp.arange(pair_count)
    own_mask = (jnp.arange(pair_total)[None, :] == own_rows[:, None]).astype(jnp.float32)
    loss_all = 0.5 * (row_lse - diag_logit) + 0.5 * (col_lse - diag_logit)
    pair_loss = jnp.dot(own_mask, loss_all, precision=lax.Precision.HIGHEST)
    prob_rows = jnp.exp(logits - row_lse[:, None])
    prob_cols = jnp.exp(logits - col_lse[None, :])
    coef = 0.5 * all_weight[:, None] * (prob_rows - eye_mat) + 0.5 * (
        prob_cols - eye_mat
    ) * all_weight[None, :]
    coef_rows = jnp.dot(own_mask, coef, precision=lax.Precision.HIGHEST)
    coef_cols = jnp.dot(own_mask, coef.T, precision=lax.Precision.HIGHEST)
    fig_grad = logit_mult * jnp.dot(
        coef_rows, all_cap.astype(jnp.float32), precision=lax.Precision.HIGHEST
    )
    cap_grad = logit_mult * jnp.dot(
        coef_cols, all_fig.astype(jnp.float32), precision=lax.Precision.HIGHEST
    )
    figure_direction = fig_inv * (
        fig_grad - fig_unit * jnp.sum(fig_unit * fig_grad, axis=1, keepdims=True)
    )
    caption_direction = cap_inv * (
        cap_grad - cap_unit * jnp.sum(cap_unit * cap_grad, axis=1, keepdims=True)
    )
    query_ct = jnp.concatenate([figure_direction, caption_direction], axis=0)
    slot_ct = lax.dot_general(
        query_onehot.astype(jnp.float32),
        query_ct,
        (((0,), (0,)), ((), ())),
        precision=lax.Precision.HIGHEST,
    )
    branch_ct = pullback(query_ct)[0]
    slot_gradient = (slot_ct + branch_ct.astype(jnp.float32)).astype(jnp.bfloat16)
    back_rows = jnp.einsum(
        "sop,sd->opd", recv_onehot, slot_gradient, preferred_element_type=jnp.float32
    ).astype(jnp.bfloat16)
    home_rows = lax.all_to_all(back_rows, "dp", split_axis=0, concat_axis=0, tiled=True)
    page_grad = jnp.einsum(
        "opk,opd->kd", send_onehot, home_rows, preferred_element_type=jnp.float32
    ).astype(jnp.bfloat16)
    return (page_grad, pair_loss)


def solution(mesh):
    return jax.shard_map(
        body,
        mesh=mesh,
        in_specs=(
            P(("dp", "fsdp"), None),
            P(("dp", "fsdp")),
            P(("dp", "fsdp"), None),
            P(None, "fsdp", None),
            P(None, "fsdp"),
            P(("dp", "fsdp")),
            P(("dp", "fsdp")),
            P(),
            P(("dp", "fsdp")),
        ),
        out_specs=(P(("dp", "fsdp"), None), P(("dp", "fsdp"))),
        check_vma=False,
    )
```

```python
import math

import jax
import jax.numpy as jnp
from jax import lax
from jax.sharding import PartitionSpec as P

HD = 64


EPSILON = 1e-06


def log_total(values, axis):
    return jnp.log(jnp.sum(jnp.exp(values), axis=axis))


def attend(query_rows, slot_row_block, qkv_mat, kv_mat, out_mat_t, query_doc, doc_row):
    query_count = query_rows.shape[0]
    row_count = slot_row_block.shape[0]
    query_h = (
        jnp.dot(query_rows, qkv_mat[0], preferred_element_type=jnp.float32)
        .astype(jnp.bfloat16)
        .reshape(query_count, -1, HD)
    )
    key_value = jnp.dot(slot_row_block, kv_mat, preferred_element_type=jnp.float32).astype(
        jnp.bfloat16
    )
    head_width = qkv_mat.shape[2]
    key_h = key_value[:, :head_width].reshape(row_count, -1, HD)
    value_h = key_value[:, head_width:].reshape(row_count, -1, HD)
    scores = jnp.einsum("qhd,khd->hqk", query_h, key_h, preferred_element_type=jnp.float32) * (
        1.0 / math.sqrt(HD)
    )
    same_doc = query_doc[:, None] == doc_row[None, :]
    scores = jnp.where(same_doc[None], scores, -1e30)
    weights = jnp.exp(scores)
    attn_prob = (weights / jnp.sum(weights, axis=2, keepdims=True)).astype(jnp.bfloat16)
    mixed = jnp.einsum("hqk,khd->qhd", attn_prob, value_h, preferred_element_type=jnp.float32)
    mixed = mixed.astype(jnp.bfloat16).reshape(query_count, -1)
    return lax.dot_general(
        mixed, out_mat_t, (((1,), (1,)), ((), ())), preferred_element_type=jnp.float32
    )


def select_rows(onehot, rows):
    picked = jnp.dot(onehot, rows, preferred_element_type=jnp.float32)
    return picked.astype(rows.dtype)


def select_rows_t(onehot, rows):
    picked = lax.dot_general(
        onehot, rows, (((0,), (0,)), ((), ())), preferred_element_type=jnp.float32
    )
    return picked.astype(rows.dtype)


def body(
    page_embed,
    page_slot,
    doc_ids,
    qkv_weight,
    out_weight,
    fig_slot,
    cap_slot,
    logit_scale,
    loss_cotangent,
):
    dp_count = lax.axis_size("dp")
    row_count = page_embed.shape[0]
    feature_width = page_embed.shape[1]
    capacity = 5 * row_count // (4 * dp_count)
    buffer_rows = dp_count * capacity
    owner_idx = page_slot // row_count
    slot_idx = page_slot % row_count
    onehot = (owner_idx[:, None] == jnp.arange(dp_count)[None, :]).astype(jnp.int32)
    rank_idx = jnp.sum((jnp.cumsum(onehot, axis=0) - onehot) * onehot, axis=1)
    dest = owner_idx * capacity + rank_idx
    send_match = dest[None, :] == jnp.arange(buffer_rows)[:, None]
    send_ids = jnp.where(
        jnp.any(send_match, axis=1),
        jnp.sum(jnp.where(send_match, slot_idx[None, :], 0), axis=1),
        row_count,
    ).reshape(dp_count, capacity)
    send_onehot = jnp.concatenate(
        [
            send_match.astype(jnp.bfloat16).reshape(dp_count, capacity, row_count),
            jnp.zeros((dp_count, 1, row_count), jnp.bfloat16),
        ],
        axis=1,
    )
    id_lanes = jnp.zeros((dp_count, feature_width), jnp.float32)
    id_lanes = id_lanes.at[:, :capacity].set((send_ids // 16).astype(jnp.float32))
    id_lanes = id_lanes.at[:, 128 : 128 + capacity].set((send_ids % 16).astype(jnp.float32))
    id_rows = jnp.concatenate(
        [jnp.zeros((dp_count, capacity, feature_width), jnp.float32), id_lanes[:, None, :]], axis=1
    )
    send_rows = (
        jnp.einsum("opk,kd->opd", send_onehot, page_embed, preferred_element_type=jnp.float32)
        + id_rows
    ).astype(jnp.bfloat16)
    recv_rows = lax.all_to_all(send_rows, "dp", split_axis=0, concat_axis=0, tiled=True)
    id_row = recv_rows[:, capacity, :].astype(jnp.float32)
    recv_ids = (
        id_row[:, :capacity].astype(jnp.int32) * 16
        + id_row[:, 128 : 128 + capacity].astype(jnp.int32)
    )
    recv_ids = jnp.concatenate([recv_ids, jnp.full((dp_count, 1), row_count, jnp.int32)], axis=1)
    recv_onehot = (
        jnp.arange(row_count)[:, None, None] == recv_ids[None, :, :]
    ).astype(jnp.bfloat16)
    slot_row_block = jnp.einsum(
        "sop,opd->sd", recv_onehot, recv_rows, preferred_element_type=jnp.float32
    ).astype(jnp.bfloat16)
    weight_stack = jnp.concatenate([qkv_weight, out_weight.T[None]], axis=0)
    weight_full = lax.all_gather(weight_stack, "fsdp", axis=1, tiled=True)
    qkv_full = weight_full[:3]
    out_full_t = weight_full[3]
    kv_full = jnp.concatenate([qkv_full[1], qkv_full[2]], axis=1)
    doc_row = doc_ids[0]
    pair_count = fig_slot.shape[0]
    query_slots = jnp.concatenate([fig_slot, cap_slot], axis=0)
    query_onehot = (query_slots[:, None] == jnp.arange(row_count)[None, :]).astype(jnp.bfloat16)
    query_doc = jnp.sum(
        jnp.where(query_slots[:, None] == jnp.arange(row_count)[None, :], doc_row[None, :], 0),
        axis=1,
    )

    def branch(inputs):
        picked = select_rows(query_onehot, inputs)
        return attend(picked, inputs, qkv_full, kv_full, out_full_t, query_doc, doc_row)

    attn_out, pullback = jax.vjp(branch, slot_row_block)
    query_rows = select_rows(query_onehot, slot_row_block)
    query_output = query_rows.astype(jnp.float32) + attn_out
    fig_vec = query_output[:pair_count]
    cap_vec = query_output[pair_count:]
    fig_inv = lax.rsqrt(jnp.sum(fig_vec * fig_vec, axis=1, keepdims=True) + EPSILON)
    cap_inv = lax.rsqrt(jnp.sum(cap_vec * cap_vec, axis=1, keepdims=True) + EPSILON)
    fig_unit = fig_vec * fig_inv
    cap_unit = cap_vec * cap_inv
    fig_emb = fig_unit.astype(jnp.bfloat16)
    cap_emb = cap_unit.astype(jnp.bfloat16)
    weight_hi = loss_cotangent.astype(jnp.bfloat16)
    weight_lo = (loss_cotangent - weight_hi.astype(jnp.float32)).astype(jnp.bfloat16)
    weight_rows = jnp.zeros((2, feature_width), jnp.bfloat16)
    weight_rows = weight_rows.at[0, :pair_count].set(weight_hi).at[1, :pair_count].set(weight_lo)
    both_emb = jnp.concatenate([fig_emb, cap_emb, weight_rows], axis=0)
    all_both = lax.all_to_all(
        jnp.broadcast_to(both_emb[None], (dp_count,) + both_emb.shape),
        "dp",
        split_axis=0,
        concat_axis=0,
        tiled=True,
    )
    all_fig = all_both[:, :pair_count].reshape(-1, feature_width)
    all_cap = all_both[:, pair_count : 2 * pair_count].reshape(-1, feature_width)
    all_weight = (
        all_both[:, 2 * pair_count, :pair_count].astype(jnp.float32)
        + all_both[:, 2 * pair_count + 1, :pair_count].astype(jnp.float32)
    ).reshape(-1)
    logit_mult = logit_scale[0]
    pair_total = all_fig.shape[0]
    first_pair = lax.axis_index("dp") * pair_count
    logits = logit_mult * jnp.dot(all_fig, all_cap.T, preferred_element_type=jnp.float32)
    row_lse = log_total(logits, 1)
    col_lse = log_total(logits, 0)
    eye_mat = jnp.eye(pair_total, dtype=jnp.float32)
    diag_logit = jnp.sum(logits * eye_mat, axis=1)
    own_rows = first_pair + jnp.arange(pair_count)
    own_mask = (jnp.arange(pair_total)[None, :] == own_rows[:, None]).astype(jnp.float32)
    loss_all = 0.5 * (row_lse - diag_logit) + 0.5 * (col_lse - diag_logit)
    pair_loss = jnp.dot(own_mask, loss_all, precision=lax.Precision.HIGHEST)
    prob_rows = jnp.exp(logits - row_lse[:, None])
    prob_cols = jnp.exp(logits - col_lse[None, :])
    coef = 0.5 * all_weight[:, None] * (prob_rows - eye_mat) + 0.5 * (
        prob_cols - eye_mat
    ) * all_weight[None, :]
    coef_rows = jnp.dot(own_mask, coef, precision=lax.Precision.HIGHEST)
    coef_cols = jnp.dot(own_mask, coef.T, precision=lax.Precision.HIGHEST)
    fig_grad = logit_mult * jnp.dot(
        coef_rows, all_cap.astype(jnp.float32), precision=lax.Precision.HIGHEST
    )
    cap_grad = logit_mult * jnp.dot(
        coef_cols, all_fig.astype(jnp.float32), precision=lax.Precision.HIGHEST
    )
    figure_direction = fig_inv * (
        fig_grad - fig_unit * jnp.sum(fig_unit * fig_grad, axis=1, keepdims=True)
    )
    caption_direction = cap_inv * (
        cap_grad - cap_unit * jnp.sum(cap_unit * cap_grad, axis=1, keepdims=True)
    )
    query_ct = jnp.concatenate([figure_direction, caption_direction], axis=0)
    slot_ct = lax.dot_general(
        query_onehot.astype(jnp.float32),
        query_ct,
        (((0,), (0,)), ((), ())),
        precision=lax.Precision.HIGHEST,
    )
    branch_ct = pullback(query_ct)[0]
    slot_gradient = (slot_ct + branch_ct.astype(jnp.float32)).astype(jnp.bfloat16)
    back_rows = jnp.einsum(
        "sop,sd->opd", recv_onehot, slot_gradient, preferred_element_type=jnp.float32
    ).astype(jnp.bfloat16)
    home_rows = lax.all_to_all(back_rows, "dp", split_axis=0, concat_axis=0, tiled=True)
    page_grad = jnp.einsum(
        "opk,opd->kd", send_onehot, home_rows, preferred_element_type=jnp.float32
    ).astype(jnp.bfloat16)
    return (page_grad, pair_loss)


def solution(mesh):
    return jax.shard_map(
        body,
        mesh=mesh,
        in_specs=(
            P(("dp", "fsdp"), None),
            P(("dp", "fsdp")),
            P(("dp", "fsdp"), None),
            P(None, "fsdp", None),
            P(None, "fsdp"),
            P(("dp", "fsdp")),
            P(("dp", "fsdp")),
            P(),
            P(("dp", "fsdp")),
        ),
        out_specs=(P(("dp", "fsdp"), None), P(("dp", "fsdp"))),
        check_vma=False,
    )
```

```python
import math

import jax
import jax.numpy as jnp
from jax import lax
from jax.sharding import PartitionSpec as P

HD = 64


EPSILON = 1e-06


def log_total(values, axis):
    return jnp.log(jnp.sum(jnp.exp(values), axis=axis))


def attend(query_h, key_value, out_mat, query_doc, doc_row):
    query_count = query_h.shape[0]
    row_count = key_value.shape[0]
    head_width = query_h.shape[1]
    query_h = query_h.reshape(query_count, -1, HD)
    key_h = key_value[:, :head_width].reshape(row_count, -1, HD)
    value_h = key_value[:, head_width:].reshape(row_count, -1, HD)
    scores = jnp.einsum("qhd,khd->hqk", query_h, key_h, preferred_element_type=jnp.float32) * (
        1.0 / math.sqrt(HD)
    )
    same_doc = query_doc[:, None] == doc_row[None, :]
    scores = jnp.where(same_doc[None], scores, -1e30)
    weights = jnp.exp(scores)
    attn_prob = (weights / jnp.sum(weights, axis=2, keepdims=True)).astype(jnp.bfloat16)
    mixed = jnp.einsum("hqk,khd->qhd", attn_prob, value_h, preferred_element_type=jnp.float32)
    mixed = mixed.astype(jnp.bfloat16).reshape(query_count, -1)
    return jnp.dot(mixed, out_mat, preferred_element_type=jnp.float32)


def select_rows(onehot, rows):
    picked = jnp.dot(onehot, rows, preferred_element_type=jnp.float32)
    return picked.astype(rows.dtype)


def select_rows_t(onehot, rows):
    picked = lax.dot_general(
        onehot, rows, (((0,), (0,)), ((), ())), preferred_element_type=jnp.float32
    )
    return picked.astype(rows.dtype)


def body(
    page_embed,
    page_slot,
    doc_ids,
    qkv_weight,
    out_weight,
    fig_slot,
    cap_slot,
    logit_scale,
    loss_cotangent,
):
    dp_count = lax.axis_size("dp")
    row_count = page_embed.shape[0]
    feature_width = page_embed.shape[1]
    capacity = 5 * row_count // (4 * dp_count)
    buffer_rows = dp_count * capacity
    owner_idx = page_slot // row_count
    slot_idx = page_slot % row_count
    onehot = (owner_idx[:, None] == jnp.arange(dp_count)[None, :]).astype(jnp.int32)
    rank_idx = jnp.sum((jnp.cumsum(onehot, axis=0) - onehot) * onehot, axis=1)
    dest = owner_idx * capacity + rank_idx
    send_match = dest[None, :] == jnp.arange(buffer_rows)[:, None]
    send_ids = jnp.where(
        jnp.any(send_match, axis=1),
        jnp.sum(jnp.where(send_match, slot_idx[None, :], 0), axis=1),
        row_count,
    ).reshape(dp_count, capacity)
    send_onehot = jnp.concatenate(
        [
            send_match.astype(jnp.bfloat16).reshape(dp_count, capacity, row_count),
            jnp.zeros((dp_count, 1, row_count), jnp.bfloat16),
        ],
        axis=1,
    )
    id_lanes = jnp.zeros((dp_count, feature_width), jnp.float32)
    id_lanes = id_lanes.at[:, :capacity].set((send_ids // 16).astype(jnp.float32))
    id_lanes = id_lanes.at[:, 128 : 128 + capacity].set((send_ids % 16).astype(jnp.float32))
    id_rows = jnp.concatenate(
        [jnp.zeros((dp_count, capacity, feature_width), jnp.float32), id_lanes[:, None, :]], axis=1
    )
    send_rows = (
        jnp.einsum("opk,kd->opd", send_onehot, page_embed, preferred_element_type=jnp.float32)
        + id_rows
    ).astype(jnp.bfloat16)
    recv_rows = lax.all_to_all(send_rows, "dp", split_axis=0, concat_axis=0, tiled=True)
    id_row = recv_rows[:, capacity, :].astype(jnp.float32)
    recv_ids = (
        id_row[:, :capacity].astype(jnp.int32) * 16
        + id_row[:, 128 : 128 + capacity].astype(jnp.int32)
    )
    recv_ids = jnp.concatenate([recv_ids, jnp.full((dp_count, 1), row_count, jnp.int32)], axis=1)
    recv_onehot = (
        jnp.arange(row_count)[:, None, None] == recv_ids[None, :, :]
    ).astype(jnp.bfloat16)
    slot_row_block = jnp.einsum(
        "sop,opd->sd", recv_onehot, recv_rows, preferred_element_type=jnp.float32
    ).astype(jnp.bfloat16)
    qkv_full, out_full = (
        lax.all_gather(qkv_weight, "fsdp", axis=1, tiled=True),
        lax.all_gather(out_weight, "fsdp", axis=1, tiled=True),
    )
    kv_full = jnp.concatenate([qkv_full[1], qkv_full[2]], axis=1)
    doc_row = doc_ids[0]
    pair_count = fig_slot.shape[0]
    query_slots = jnp.concatenate([fig_slot, cap_slot], axis=0)
    query_onehot = (query_slots[:, None] == jnp.arange(row_count)[None, :]).astype(jnp.bfloat16)
    query_doc = jnp.sum(
        jnp.where(query_slots[:, None] == jnp.arange(row_count)[None, :], doc_row[None, :], 0),
        axis=1,
    )

    query_rows = select_rows(query_onehot, slot_row_block)
    query_h = jnp.dot(query_rows, qkv_full[0], preferred_element_type=jnp.float32).astype(
        jnp.bfloat16
    )
    key_value = jnp.dot(slot_row_block, kv_full, preferred_element_type=jnp.float32).astype(
        jnp.bfloat16
    )

    def branch(query_in, key_value_in):
        return attend(query_in, key_value_in, out_full, query_doc, doc_row)

    attn_out, pullback = jax.vjp(branch, query_h, key_value)
    query_output = query_rows.astype(jnp.float32) + attn_out
    fig_vec = query_output[:pair_count]
    cap_vec = query_output[pair_count:]
    fig_inv = lax.rsqrt(jnp.sum(fig_vec * fig_vec, axis=1, keepdims=True) + EPSILON)
    cap_inv = lax.rsqrt(jnp.sum(cap_vec * cap_vec, axis=1, keepdims=True) + EPSILON)
    fig_unit = fig_vec * fig_inv
    cap_unit = cap_vec * cap_inv
    fig_emb = fig_unit.astype(jnp.bfloat16)
    cap_emb = cap_unit.astype(jnp.bfloat16)
    weight_hi = loss_cotangent.astype(jnp.bfloat16)
    weight_lo = (loss_cotangent - weight_hi.astype(jnp.float32)).astype(jnp.bfloat16)
    weight_rows = jnp.zeros((2, feature_width), jnp.bfloat16)
    weight_rows = weight_rows.at[0, :pair_count].set(weight_hi).at[1, :pair_count].set(weight_lo)
    both_emb = jnp.concatenate([fig_emb, cap_emb, weight_rows], axis=0)
    all_both = lax.all_to_all(
        jnp.broadcast_to(both_emb[None], (dp_count,) + both_emb.shape),
        "dp",
        split_axis=0,
        concat_axis=0,
        tiled=True,
    )
    all_fig = all_both[:, :pair_count].reshape(-1, feature_width)
    all_cap = all_both[:, pair_count : 2 * pair_count].reshape(-1, feature_width)
    all_weight = (
        all_both[:, 2 * pair_count, :pair_count].astype(jnp.float32)
        + all_both[:, 2 * pair_count + 1, :pair_count].astype(jnp.float32)
    ).reshape(-1)
    logit_mult = logit_scale[0]
    pair_total = all_fig.shape[0]
    first_pair = lax.axis_index("dp") * pair_count
    logits = logit_mult * jnp.dot(all_fig, all_cap.T, preferred_element_type=jnp.float32)
    row_lse = log_total(logits, 1)
    col_lse = log_total(logits, 0)
    eye_mat = jnp.eye(pair_total, dtype=jnp.float32)
    diag_logit = jnp.sum(logits * eye_mat, axis=1)
    own_rows = first_pair + jnp.arange(pair_count)
    own_mask = (jnp.arange(pair_total)[None, :] == own_rows[:, None]).astype(jnp.float32)
    loss_all = 0.5 * (row_lse - diag_logit) + 0.5 * (col_lse - diag_logit)
    pair_loss = jnp.dot(own_mask, loss_all, precision=lax.Precision.HIGHEST)
    prob_rows = jnp.exp(logits - row_lse[:, None])
    prob_cols = jnp.exp(logits - col_lse[None, :])
    coef = 0.5 * all_weight[:, None] * (prob_rows - eye_mat) + 0.5 * (
        prob_cols - eye_mat
    ) * all_weight[None, :]
    coef_rows = jnp.dot(own_mask, coef, precision=lax.Precision.HIGHEST)
    coef_cols = jnp.dot(own_mask, coef.T, precision=lax.Precision.HIGHEST)
    fig_grad = logit_mult * jnp.dot(
        coef_rows, all_cap.astype(jnp.float32), precision=lax.Precision.HIGHEST
    )
    cap_grad = logit_mult * jnp.dot(
        coef_cols, all_fig.astype(jnp.float32), precision=lax.Precision.HIGHEST
    )
    figure_direction = fig_inv * (
        fig_grad - fig_unit * jnp.sum(fig_unit * fig_grad, axis=1, keepdims=True)
    )
    caption_direction = cap_inv * (
        cap_grad - cap_unit * jnp.sum(cap_unit * cap_grad, axis=1, keepdims=True)
    )
    query_ct = jnp.concatenate([figure_direction, caption_direction], axis=0)
    query_ct_rows, key_value_ct = pullback(query_ct)
    half = feature_width // 2
    grad_parts = []
    for part in range(2):
        cols = slice(part * half, (part + 1) * half)
        query_part = lax.dot_general(
            query_ct_rows,
            qkv_full[0][cols],
            (((1,), (1,)), ((), ())),
            preferred_element_type=jnp.float32,
        )
        slot_part = lax.dot_general(
            key_value_ct,
            kv_full[cols],
            (((1,), (1,)), ((), ())),
            preferred_element_type=jnp.float32,
        )
        scatter_part = lax.dot_general(
            query_onehot.astype(jnp.float32),
            query_part + query_ct[:, cols],
            (((0,), (0,)), ((), ())),
            precision=lax.Precision.HIGHEST,
        )
        slot_gradient = (slot_part + scatter_part).astype(jnp.bfloat16)
        back_rows = jnp.einsum(
            "sop,sd->opd", recv_onehot, slot_gradient, preferred_element_type=jnp.float32
        ).astype(jnp.bfloat16)
        home_rows = lax.all_to_all(back_rows, "dp", split_axis=0, concat_axis=0, tiled=True)
        grad_parts.append(
            jnp.einsum(
                "opk,opd->kd", send_onehot, home_rows, preferred_element_type=jnp.float32
            ).astype(jnp.bfloat16)
        )
    page_grad = jnp.concatenate(grad_parts, axis=1)
    return (page_grad, pair_loss)


def solution(mesh):
    return jax.shard_map(
        body,
        mesh=mesh,
        in_specs=(
            P(("dp", "fsdp"), None),
            P(("dp", "fsdp")),
            P(("dp", "fsdp"), None),
            P(None, "fsdp", None),
            P(None, "fsdp"),
            P(("dp", "fsdp")),
            P(("dp", "fsdp")),
            P(),
            P(("dp", "fsdp")),
        ),
        out_specs=(P(("dp", "fsdp"), None), P(("dp", "fsdp"))),
        check_vma=False,
    )
```

```python
import math

import jax
import jax.numpy as jnp
from jax import lax
from jax.sharding import PartitionSpec as P

HD = 64


EPSILON = 1e-06


def log_total(values, axis):
    return jnp.log(jnp.sum(jnp.exp(values), axis=axis))


def attend(query_h, key_value, out_mat, query_doc, doc_row):
    query_count = query_h.shape[0]
    row_count = key_value.shape[0]
    head_width = query_h.shape[1]
    query_h = query_h.reshape(query_count, -1, HD)
    key_h = key_value[:, :head_width].reshape(row_count, -1, HD)
    value_h = key_value[:, head_width:].reshape(row_count, -1, HD)
    scores = jnp.einsum("qhd,khd->hqk", query_h, key_h, preferred_element_type=jnp.float32) * (
        1.0 / math.sqrt(HD)
    )
    same_doc = query_doc[:, None] == doc_row[None, :]
    scores = jnp.where(same_doc[None], scores, -1e30)
    weights = jnp.exp(scores)
    attn_prob = (weights / jnp.sum(weights, axis=2, keepdims=True)).astype(jnp.bfloat16)
    mixed = jnp.einsum("hqk,khd->qhd", attn_prob, value_h, preferred_element_type=jnp.float32)
    mixed = mixed.astype(jnp.bfloat16).reshape(query_count, -1)
    return jnp.dot(mixed, out_mat, preferred_element_type=jnp.float32)


def select_rows(onehot, rows):
    picked = jnp.dot(onehot, rows, preferred_element_type=jnp.float32)
    return picked.astype(rows.dtype)


def select_rows_t(onehot, rows):
    picked = lax.dot_general(
        onehot, rows, (((0,), (0,)), ((), ())), preferred_element_type=jnp.float32
    )
    return picked.astype(rows.dtype)


def body(
    page_embed,
    page_slot,
    doc_ids,
    qkv_weight,
    out_weight,
    fig_slot,
    cap_slot,
    logit_scale,
    loss_cotangent,
):
    dp_count = lax.axis_size("dp")
    row_count = page_embed.shape[0]
    feature_width = page_embed.shape[1]
    capacity = 5 * row_count // (4 * dp_count)
    buffer_rows = dp_count * capacity
    owner_idx = page_slot // row_count
    slot_idx = page_slot % row_count
    onehot = (owner_idx[:, None] == jnp.arange(dp_count)[None, :]).astype(jnp.int32)
    rank_idx = jnp.sum((jnp.cumsum(onehot, axis=0) - onehot) * onehot, axis=1)
    dest = owner_idx * capacity + rank_idx
    send_match = dest[None, :] == jnp.arange(buffer_rows)[:, None]
    send_ids = jnp.where(
        jnp.any(send_match, axis=1),
        jnp.sum(jnp.where(send_match, slot_idx[None, :], 0), axis=1),
        row_count,
    ).reshape(dp_count, capacity)
    send_onehot = jnp.concatenate(
        [
            send_match.astype(jnp.bfloat16).reshape(dp_count, capacity, row_count),
            jnp.zeros((dp_count, 1, row_count), jnp.bfloat16),
        ],
        axis=1,
    )
    id_lanes = jnp.zeros((dp_count, feature_width), jnp.float32)
    id_lanes = id_lanes.at[:, :capacity].set((send_ids // 16).astype(jnp.float32))
    id_lanes = id_lanes.at[:, 128 : 128 + capacity].set((send_ids % 16).astype(jnp.float32))
    id_rows = jnp.concatenate(
        [jnp.zeros((dp_count, capacity, feature_width), jnp.float32), id_lanes[:, None, :]], axis=1
    )
    send_rows = (
        jnp.einsum("opk,kd->opd", send_onehot, page_embed, preferred_element_type=jnp.float32)
        + id_rows
    ).astype(jnp.bfloat16)
    recv_rows = lax.all_to_all(send_rows, "dp", split_axis=0, concat_axis=0, tiled=True)
    id_row = recv_rows[:, capacity, :].astype(jnp.float32)
    recv_ids = (
        id_row[:, :capacity].astype(jnp.int32) * 16
        + id_row[:, 128 : 128 + capacity].astype(jnp.int32)
    )
    recv_ids = jnp.concatenate([recv_ids, jnp.full((dp_count, 1), row_count, jnp.int32)], axis=1)
    recv_onehot = (
        jnp.arange(row_count)[:, None, None] == recv_ids[None, :, :]
    ).astype(jnp.bfloat16)
    slot_row_block = jnp.einsum(
        "sop,opd->sd", recv_onehot, recv_rows, preferred_element_type=jnp.float32
    ).astype(jnp.bfloat16)
    qkv_full, out_full = (
        lax.all_gather(qkv_weight, "fsdp", axis=1, tiled=True),
        lax.all_gather(out_weight, "fsdp", axis=1, tiled=True),
    )
    kv_full = jnp.concatenate([qkv_full[1], qkv_full[2]], axis=1)
    doc_row = doc_ids[0]
    pair_count = fig_slot.shape[0]
    query_slots = jnp.concatenate([fig_slot, cap_slot], axis=0)
    query_onehot = (query_slots[:, None] == jnp.arange(row_count)[None, :]).astype(jnp.bfloat16)
    query_doc = jnp.sum(
        jnp.where(query_slots[:, None] == jnp.arange(row_count)[None, :], doc_row[None, :], 0),
        axis=1,
    )

    query_rows = select_rows(query_onehot, slot_row_block)
    query_h = jnp.dot(query_rows, qkv_full[0], preferred_element_type=jnp.float32).astype(
        jnp.bfloat16
    )
    key_value = jnp.dot(slot_row_block, kv_full, preferred_element_type=jnp.float32).astype(
        jnp.bfloat16
    )

    def branch(query_in, key_value_in):
        return attend(query_in, key_value_in, out_full, query_doc, doc_row)

    attn_out, pullback = jax.vjp(branch, query_h, key_value)
    query_output = query_rows.astype(jnp.float32) + attn_out
    fig_vec = query_output[:pair_count]
    cap_vec = query_output[pair_count:]
    fig_inv = lax.rsqrt(jnp.sum(fig_vec * fig_vec, axis=1, keepdims=True) + EPSILON)
    cap_inv = lax.rsqrt(jnp.sum(cap_vec * cap_vec, axis=1, keepdims=True) + EPSILON)
    fig_unit = fig_vec * fig_inv
    cap_unit = cap_vec * cap_inv
    fig_emb = fig_unit.astype(jnp.bfloat16)
    cap_emb = cap_unit.astype(jnp.bfloat16)
    weight_hi = loss_cotangent.astype(jnp.bfloat16)
    weight_lo = (loss_cotangent - weight_hi.astype(jnp.float32)).astype(jnp.bfloat16)
    weight_rows = jnp.zeros((2, feature_width), jnp.bfloat16)
    weight_rows = weight_rows.at[0, :pair_count].set(weight_hi).at[1, :pair_count].set(weight_lo)
    both_emb = jnp.concatenate([fig_emb, cap_emb, weight_rows], axis=0)
    all_both = lax.all_to_all(
        jnp.broadcast_to(both_emb[None], (dp_count,) + both_emb.shape),
        "dp",
        split_axis=0,
        concat_axis=0,
        tiled=True,
    )
    all_fig = all_both[:, :pair_count].reshape(-1, feature_width)
    all_cap = all_both[:, pair_count : 2 * pair_count].reshape(-1, feature_width)
    all_weight = (
        all_both[:, 2 * pair_count, :pair_count].astype(jnp.float32)
        + all_both[:, 2 * pair_count + 1, :pair_count].astype(jnp.float32)
    ).reshape(-1)
    logit_mult = logit_scale[0]
    pair_total = all_fig.shape[0]
    first_pair = lax.axis_index("dp") * pair_count
    logits = logit_mult * jnp.dot(all_fig, all_cap.T, preferred_element_type=jnp.float32)
    row_lse = log_total(logits, 1)
    col_lse = log_total(logits, 0)
    eye_mat = jnp.eye(pair_total, dtype=jnp.float32)
    diag_logit = jnp.sum(logits * eye_mat, axis=1)
    own_rows = first_pair + jnp.arange(pair_count)
    own_mask = (jnp.arange(pair_total)[None, :] == own_rows[:, None]).astype(jnp.float32)
    loss_all = 0.5 * (row_lse - diag_logit) + 0.5 * (col_lse - diag_logit)
    pair_loss = jnp.dot(own_mask, loss_all, precision=lax.Precision.HIGHEST)
    prob_rows = jnp.exp(logits - row_lse[:, None])
    prob_cols = jnp.exp(logits - col_lse[None, :])
    coef = 0.5 * all_weight[:, None] * (prob_rows - eye_mat) + 0.5 * (
        prob_cols - eye_mat
    ) * all_weight[None, :]
    coef_rows = jnp.dot(own_mask, coef, precision=lax.Precision.HIGHEST)
    coef_cols = jnp.dot(own_mask, coef.T, precision=lax.Precision.HIGHEST)
    fig_grad = logit_mult * jnp.dot(
        coef_rows, all_cap.astype(jnp.float32), precision=lax.Precision.HIGHEST
    )
    cap_grad = logit_mult * jnp.dot(
        coef_cols, all_fig.astype(jnp.float32), precision=lax.Precision.HIGHEST
    )
    figure_direction = fig_inv * (
        fig_grad - fig_unit * jnp.sum(fig_unit * fig_grad, axis=1, keepdims=True)
    )
    caption_direction = cap_inv * (
        cap_grad - cap_unit * jnp.sum(cap_unit * cap_grad, axis=1, keepdims=True)
    )
    query_ct = jnp.concatenate([figure_direction, caption_direction], axis=0)
    query_ct_rows, key_value_ct = pullback(query_ct)
    first_width = feature_width // 4
    grad_parts = []
    for cols in (slice(0, first_width), slice(first_width, feature_width)):
        query_part = lax.dot_general(
            query_ct_rows,
            qkv_full[0][cols],
            (((1,), (1,)), ((), ())),
            preferred_element_type=jnp.float32,
        )
        slot_part = lax.dot_general(
            key_value_ct,
            kv_full[cols],
            (((1,), (1,)), ((), ())),
            preferred_element_type=jnp.float32,
        )
        scatter_part = lax.dot_general(
            query_onehot.astype(jnp.float32),
            query_part + query_ct[:, cols],
            (((0,), (0,)), ((), ())),
            precision=lax.Precision.HIGHEST,
        )
        slot_gradient = (slot_part + scatter_part).astype(jnp.bfloat16)
        back_rows = jnp.einsum(
            "sop,sd->opd", recv_onehot, slot_gradient, preferred_element_type=jnp.float32
        ).astype(jnp.bfloat16)
        home_rows = lax.all_to_all(back_rows, "dp", split_axis=0, concat_axis=0, tiled=True)
        grad_parts.append(
            jnp.einsum(
                "opk,opd->kd", send_onehot, home_rows, preferred_element_type=jnp.float32
            ).astype(jnp.bfloat16)
        )
    page_grad = jnp.concatenate(grad_parts, axis=1)
    return (page_grad, pair_loss)


def solution(mesh):
    return jax.shard_map(
        body,
        mesh=mesh,
        in_specs=(
            P(("dp", "fsdp"), None),
            P(("dp", "fsdp")),
            P(("dp", "fsdp"), None),
            P(None, "fsdp", None),
            P(None, "fsdp"),
            P(("dp", "fsdp")),
            P(("dp", "fsdp")),
            P(),
            P(("dp", "fsdp")),
        ),
        out_specs=(P(("dp", "fsdp"), None), P(("dp", "fsdp"))),
        check_vma=False,
    )
```

```python
import math

import jax
import jax.numpy as jnp
from jax import lax
from jax.sharding import PartitionSpec as P

HD = 64


EPSILON = 1e-06


def log_total(values, axis):
    return jnp.log(jnp.sum(jnp.exp(values), axis=axis))


def attend(query_h, key_value, out_mat, query_doc, doc_row):
    query_count = query_h.shape[0]
    row_count = key_value.shape[0]
    head_width = query_h.shape[1]
    query_h = query_h.reshape(query_count, -1, HD)
    key_h = key_value[:, :head_width].reshape(row_count, -1, HD)
    value_h = key_value[:, head_width:].reshape(row_count, -1, HD)
    scores = jnp.einsum("qhd,khd->hqk", query_h, key_h, preferred_element_type=jnp.float32) * (
        1.0 / math.sqrt(HD)
    )
    same_doc = query_doc[:, None] == doc_row[None, :]
    scores = jnp.where(same_doc[None], scores, -1e30)
    weights = jnp.exp(scores)
    attn_prob = (weights / jnp.sum(weights, axis=2, keepdims=True)).astype(jnp.bfloat16)
    mixed = jnp.einsum("hqk,khd->qhd", attn_prob, value_h, preferred_element_type=jnp.float32)
    mixed = mixed.astype(jnp.bfloat16).reshape(query_count, -1)
    return jnp.dot(mixed, out_mat, preferred_element_type=jnp.float32)


def select_rows(onehot, rows):
    picked = jnp.dot(onehot, rows, preferred_element_type=jnp.float32)
    return picked.astype(rows.dtype)


def select_rows_t(onehot, rows):
    picked = lax.dot_general(
        onehot, rows, (((0,), (0,)), ((), ())), preferred_element_type=jnp.float32
    )
    return picked.astype(rows.dtype)


def body(
    page_embed,
    page_slot,
    doc_ids,
    qkv_weight,
    out_weight,
    fig_slot,
    cap_slot,
    logit_scale,
    loss_cotangent,
):
    dp_count = lax.axis_size("dp")
    row_count = page_embed.shape[0]
    feature_width = page_embed.shape[1]
    capacity = 5 * row_count // (4 * dp_count)
    buffer_rows = dp_count * capacity
    owner_idx = page_slot // row_count
    slot_idx = page_slot % row_count
    onehot = (owner_idx[:, None] == jnp.arange(dp_count)[None, :]).astype(jnp.int32)
    rank_idx = jnp.sum((jnp.cumsum(onehot, axis=0) - onehot) * onehot, axis=1)
    dest = owner_idx * capacity + rank_idx
    send_match = dest[None, :] == jnp.arange(buffer_rows)[:, None]
    send_ids = jnp.where(
        jnp.any(send_match, axis=1),
        jnp.sum(jnp.where(send_match, slot_idx[None, :], 0), axis=1),
        row_count,
    ).reshape(dp_count, capacity)
    send_onehot = jnp.concatenate(
        [
            send_match.astype(jnp.bfloat16).reshape(dp_count, capacity, row_count),
            jnp.zeros((dp_count, 1, row_count), jnp.bfloat16),
        ],
        axis=1,
    )
    id_lanes = jnp.zeros((dp_count, feature_width), jnp.float32)
    id_lanes = id_lanes.at[:, :capacity].set((send_ids // 16).astype(jnp.float32))
    id_lanes = id_lanes.at[:, 128 : 128 + capacity].set((send_ids % 16).astype(jnp.float32))
    id_rows = jnp.concatenate(
        [jnp.zeros((dp_count, capacity, feature_width), jnp.float32), id_lanes[:, None, :]], axis=1
    )
    send_rows = (
        jnp.einsum("opk,kd->opd", send_onehot, page_embed, preferred_element_type=jnp.float32)
        + id_rows
    ).astype(jnp.bfloat16)
    recv_rows = lax.all_to_all(send_rows, "dp", split_axis=0, concat_axis=0, tiled=True)
    id_row = recv_rows[:, capacity, :].astype(jnp.float32)
    recv_ids = (
        id_row[:, :capacity].astype(jnp.int32) * 16
        + id_row[:, 128 : 128 + capacity].astype(jnp.int32)
    )
    recv_ids = jnp.concatenate([recv_ids, jnp.full((dp_count, 1), row_count, jnp.int32)], axis=1)
    recv_onehot = (
        jnp.arange(row_count)[:, None, None] == recv_ids[None, :, :]
    ).astype(jnp.bfloat16)
    slot_row_block = jnp.einsum(
        "sop,opd->sd", recv_onehot, recv_rows, preferred_element_type=jnp.float32
    ).astype(jnp.bfloat16)
    qkv_full, out_full = (
        lax.all_gather(qkv_weight, "fsdp", axis=1, tiled=True),
        lax.all_gather(out_weight, "fsdp", axis=1, tiled=True),
    )
    kv_full = jnp.concatenate([qkv_full[1], qkv_full[2]], axis=1)
    doc_row = doc_ids[0]
    pair_count = fig_slot.shape[0]
    query_slots = jnp.concatenate([fig_slot, cap_slot], axis=0)
    query_onehot = (query_slots[:, None] == jnp.arange(row_count)[None, :]).astype(jnp.bfloat16)
    query_doc = jnp.sum(
        jnp.where(query_slots[:, None] == jnp.arange(row_count)[None, :], doc_row[None, :], 0),
        axis=1,
    )

    query_rows = select_rows(query_onehot, slot_row_block)
    query_h = jnp.dot(query_rows, qkv_full[0], preferred_element_type=jnp.float32).astype(
        jnp.bfloat16
    )
    key_value = jnp.dot(slot_row_block, kv_full, preferred_element_type=jnp.float32).astype(
        jnp.bfloat16
    )

    def branch(query_in, key_value_in):
        return attend(query_in, key_value_in, out_full, query_doc, doc_row)

    attn_out, pullback = jax.vjp(branch, query_h, key_value)
    query_output = query_rows.astype(jnp.float32) + attn_out
    fig_vec = query_output[:pair_count]
    cap_vec = query_output[pair_count:]
    fig_inv = lax.rsqrt(jnp.sum(fig_vec * fig_vec, axis=1, keepdims=True) + EPSILON)
    cap_inv = lax.rsqrt(jnp.sum(cap_vec * cap_vec, axis=1, keepdims=True) + EPSILON)
    fig_unit = fig_vec * fig_inv
    cap_unit = cap_vec * cap_inv
    fig_emb = fig_unit.astype(jnp.bfloat16)
    cap_emb = cap_unit.astype(jnp.bfloat16)
    weight_hi = loss_cotangent.astype(jnp.bfloat16)
    weight_lo = (loss_cotangent - weight_hi.astype(jnp.float32)).astype(jnp.bfloat16)
    weight_lanes = jnp.zeros((2 * pair_count, 128), jnp.bfloat16)
    weight_lanes = weight_lanes.at[:pair_count, 0].set(weight_hi).at[:pair_count, 1].set(weight_lo)
    both_emb = jnp.concatenate(
        [jnp.concatenate([fig_emb, cap_emb], axis=0), weight_lanes], axis=1
    )
    all_both = lax.all_to_all(
        jnp.broadcast_to(both_emb[None], (dp_count,) + both_emb.shape),
        "dp",
        split_axis=0,
        concat_axis=0,
        tiled=True,
    )
    all_fig = all_both[:, :pair_count, :feature_width].reshape(-1, feature_width)
    all_cap = all_both[:, pair_count:, :feature_width].reshape(-1, feature_width)
    all_weight = (
        all_both[:, :pair_count, feature_width].astype(jnp.float32)
        + all_both[:, :pair_count, feature_width + 1].astype(jnp.float32)
    ).reshape(-1)
    logit_mult = logit_scale[0]
    pair_total = all_fig.shape[0]
    first_pair = lax.axis_index("dp") * pair_count
    logits = logit_mult * jnp.dot(all_fig, all_cap.T, preferred_element_type=jnp.float32)
    row_lse = log_total(logits, 1)
    col_lse = log_total(logits, 0)
    eye_mat = jnp.eye(pair_total, dtype=jnp.float32)
    diag_logit = jnp.sum(logits * eye_mat, axis=1)
    own_rows = first_pair + jnp.arange(pair_count)
    own_mask = (jnp.arange(pair_total)[None, :] == own_rows[:, None]).astype(jnp.float32)
    loss_all = 0.5 * (row_lse - diag_logit) + 0.5 * (col_lse - diag_logit)
    pair_loss = jnp.dot(own_mask, loss_all, precision=lax.Precision.HIGHEST)
    prob_rows = jnp.exp(logits - row_lse[:, None])
    prob_cols = jnp.exp(logits - col_lse[None, :])
    coef = 0.5 * all_weight[:, None] * (prob_rows - eye_mat) + 0.5 * (
        prob_cols - eye_mat
    ) * all_weight[None, :]
    coef_rows = jnp.dot(own_mask, coef, precision=lax.Precision.HIGHEST)
    coef_cols = jnp.dot(own_mask, coef.T, precision=lax.Precision.HIGHEST)
    fig_grad = logit_mult * jnp.dot(
        coef_rows, all_cap.astype(jnp.float32), precision=lax.Precision.HIGHEST
    )
    cap_grad = logit_mult * jnp.dot(
        coef_cols, all_fig.astype(jnp.float32), precision=lax.Precision.HIGHEST
    )
    figure_direction = fig_inv * (
        fig_grad - fig_unit * jnp.sum(fig_unit * fig_grad, axis=1, keepdims=True)
    )
    caption_direction = cap_inv * (
        cap_grad - cap_unit * jnp.sum(cap_unit * cap_grad, axis=1, keepdims=True)
    )
    query_ct = jnp.concatenate([figure_direction, caption_direction], axis=0)
    query_ct_rows, key_value_ct = pullback(query_ct)
    half = feature_width // 2
    grad_parts = []
    for part in range(2):
        cols = slice(part * half, (part + 1) * half)
        query_part = lax.dot_general(
            query_ct_rows,
            qkv_full[0][cols],
            (((1,), (1,)), ((), ())),
            preferred_element_type=jnp.float32,
        )
        slot_part = lax.dot_general(
            key_value_ct,
            kv_full[cols],
            (((1,), (1,)), ((), ())),
            preferred_element_type=jnp.float32,
        )
        scatter_part = lax.dot_general(
            query_onehot.astype(jnp.float32),
            query_part + query_ct[:, cols],
            (((0,), (0,)), ((), ())),
            precision=lax.Precision.HIGHEST,
        )
        slot_gradient = (slot_part + scatter_part).astype(jnp.bfloat16)
        back_rows = jnp.einsum(
            "sop,sd->opd", recv_onehot, slot_gradient, preferred_element_type=jnp.float32
        ).astype(jnp.bfloat16)
        home_rows = lax.all_to_all(back_rows, "dp", split_axis=0, concat_axis=0, tiled=True)
        grad_parts.append(
            jnp.einsum(
                "opk,opd->kd", send_onehot, home_rows, preferred_element_type=jnp.float32
            ).astype(jnp.bfloat16)
        )
    page_grad = jnp.concatenate(grad_parts, axis=1)
    return (page_grad, pair_loss)


def solution(mesh):
    return jax.shard_map(
        body,
        mesh=mesh,
        in_specs=(
            P(("dp", "fsdp"), None),
            P(("dp", "fsdp")),
            P(("dp", "fsdp"), None),
            P(None, "fsdp", None),
            P(None, "fsdp"),
            P(("dp", "fsdp")),
            P(("dp", "fsdp")),
            P(),
            P(("dp", "fsdp")),
        ),
        out_specs=(P(("dp", "fsdp"), None), P(("dp", "fsdp"))),
        check_vma=False,
    )
```

```python
import math

import jax
import jax.numpy as jnp
from jax import lax
from jax.sharding import PartitionSpec as P

HD = 64


EPSILON = 1e-06


def log_total(values, axis):
    return jnp.log(jnp.sum(jnp.exp(values), axis=axis))


def attend(query_h, key_value, out_mat, query_doc, doc_row):
    query_count = query_h.shape[0]
    row_count = key_value.shape[0]
    head_width = query_h.shape[1]
    query_h = query_h.reshape(query_count, -1, HD)
    key_h = key_value[:, :head_width].reshape(row_count, -1, HD)
    value_h = key_value[:, head_width:].reshape(row_count, -1, HD)
    scores = jnp.einsum("qhd,khd->hqk", query_h, key_h, preferred_element_type=jnp.float32) * (
        1.0 / math.sqrt(HD)
    )
    same_doc = query_doc[:, None] == doc_row[None, :]
    scores = jnp.where(same_doc[None], scores, -1e30)
    weights = jnp.exp(scores)
    attn_prob = (weights / jnp.sum(weights, axis=2, keepdims=True)).astype(jnp.bfloat16)
    mixed = jnp.einsum("hqk,khd->qhd", attn_prob, value_h, preferred_element_type=jnp.float32)
    mixed = mixed.astype(jnp.bfloat16).reshape(query_count, -1)
    return jnp.dot(mixed, out_mat, preferred_element_type=jnp.float32)


def select_rows(onehot, rows):
    picked = jnp.dot(onehot, rows, preferred_element_type=jnp.float32)
    return picked.astype(rows.dtype)


def select_rows_t(onehot, rows):
    picked = lax.dot_general(
        onehot, rows, (((0,), (0,)), ((), ())), preferred_element_type=jnp.float32
    )
    return picked.astype(rows.dtype)


def body(
    page_embed,
    page_slot,
    doc_ids,
    qkv_weight,
    out_weight,
    fig_slot,
    cap_slot,
    logit_scale,
    loss_cotangent,
):
    dp_count = lax.axis_size("dp")
    row_count = page_embed.shape[0]
    feature_width = page_embed.shape[1]
    capacity = 5 * row_count // (4 * dp_count)
    buffer_rows = dp_count * capacity
    owner_idx = page_slot // row_count
    slot_idx = page_slot % row_count
    onehot = (owner_idx[:, None] == jnp.arange(dp_count)[None, :]).astype(jnp.int32)
    rank_idx = jnp.sum((jnp.cumsum(onehot, axis=0) - onehot) * onehot, axis=1)
    dest = owner_idx * capacity + rank_idx
    send_match = dest[None, :] == jnp.arange(buffer_rows)[:, None]
    send_ids = jnp.where(
        jnp.any(send_match, axis=1),
        jnp.sum(jnp.where(send_match, slot_idx[None, :], 0), axis=1),
        row_count,
    ).reshape(dp_count, capacity)
    send_onehot = jnp.concatenate(
        [
            send_match.astype(jnp.bfloat16).reshape(dp_count, capacity, row_count),
            jnp.zeros((dp_count, 1, row_count), jnp.bfloat16),
        ],
        axis=1,
    )
    id_lanes = jnp.zeros((dp_count, feature_width), jnp.float32)
    id_lanes = id_lanes.at[:, :capacity].set((send_ids // 16).astype(jnp.float32))
    id_lanes = id_lanes.at[:, 128 : 128 + capacity].set((send_ids % 16).astype(jnp.float32))
    id_rows = jnp.concatenate(
        [jnp.zeros((dp_count, capacity, feature_width), jnp.float32), id_lanes[:, None, :]], axis=1
    )
    send_rows = (
        jnp.einsum("opk,kd->opd", send_onehot, page_embed, preferred_element_type=jnp.float32)
        + id_rows
    ).astype(jnp.bfloat16)
    recv_rows = lax.all_to_all(send_rows, "dp", split_axis=0, concat_axis=0, tiled=True)
    id_row = recv_rows[:, capacity, :].astype(jnp.float32)
    recv_ids = (
        id_row[:, :capacity].astype(jnp.int32) * 16
        + id_row[:, 128 : 128 + capacity].astype(jnp.int32)
    )
    recv_ids = jnp.concatenate([recv_ids, jnp.full((dp_count, 1), row_count, jnp.int32)], axis=1)
    recv_onehot = (
        jnp.arange(row_count)[:, None, None] == recv_ids[None, :, :]
    ).astype(jnp.bfloat16)
    slot_row_block = jnp.einsum(
        "sop,opd->sd", recv_onehot, recv_rows, preferred_element_type=jnp.float32
    ).astype(jnp.bfloat16)
    qkv_full, out_full = (
        lax.all_gather(qkv_weight, "fsdp", axis=1, tiled=True),
        lax.all_gather(out_weight, "fsdp", axis=1, tiled=True),
    )
    kv_full = jnp.concatenate([qkv_full[1], qkv_full[2]], axis=1)
    doc_row = doc_ids[0]
    pair_count = fig_slot.shape[0]
    query_slots = jnp.concatenate([fig_slot, cap_slot], axis=0)
    query_onehot = (query_slots[:, None] == jnp.arange(row_count)[None, :]).astype(jnp.bfloat16)
    query_doc = jnp.sum(
        jnp.where(query_slots[:, None] == jnp.arange(row_count)[None, :], doc_row[None, :], 0),
        axis=1,
    )

    query_rows = select_rows(query_onehot, slot_row_block)
    query_h = jnp.dot(query_rows, qkv_full[0], preferred_element_type=jnp.float32).astype(
        jnp.bfloat16
    )
    key_value = jnp.dot(slot_row_block, kv_full, preferred_element_type=jnp.float32).astype(
        jnp.bfloat16
    )

    def branch(query_in, key_value_in):
        return attend(query_in, key_value_in, out_full, query_doc, doc_row)

    attn_out, pullback = jax.vjp(branch, query_h, key_value)
    query_output = query_rows.astype(jnp.float32) + attn_out
    fig_vec = query_output[:pair_count]
    cap_vec = query_output[pair_count:]
    fig_inv = lax.rsqrt(jnp.sum(fig_vec * fig_vec, axis=1, keepdims=True) + EPSILON)
    cap_inv = lax.rsqrt(jnp.sum(cap_vec * cap_vec, axis=1, keepdims=True) + EPSILON)
    fig_unit = fig_vec * fig_inv
    cap_unit = cap_vec * cap_inv
    fig_emb = fig_unit.astype(jnp.bfloat16)
    cap_emb = cap_unit.astype(jnp.bfloat16)
    weight_hi = loss_cotangent.astype(jnp.bfloat16)
    weight_lo = (loss_cotangent - weight_hi.astype(jnp.float32)).astype(jnp.bfloat16)
    weight_lanes = jnp.zeros((2 * pair_count, 128), jnp.bfloat16)
    weight_lanes = weight_lanes.at[:pair_count, 0].set(weight_hi).at[:pair_count, 1].set(weight_lo)
    both_emb = jnp.concatenate(
        [jnp.concatenate([fig_emb, cap_emb], axis=0), weight_lanes], axis=1
    )
    all_both = lax.all_to_all(
        jnp.broadcast_to(both_emb[None], (dp_count,) + both_emb.shape),
        "dp",
        split_axis=0,
        concat_axis=0,
        tiled=True,
    )
    all_fig = all_both[:, :pair_count, :feature_width].reshape(-1, feature_width)
    all_cap = all_both[:, pair_count:, :feature_width].reshape(-1, feature_width)
    all_weight = (
        all_both[:, :pair_count, feature_width].astype(jnp.float32)
        + all_both[:, :pair_count, feature_width + 1].astype(jnp.float32)
    ).reshape(-1)
    logit_mult = logit_scale[0]
    pair_total = all_fig.shape[0]
    first_pair = lax.axis_index("dp") * pair_count
    logits = logit_mult * jnp.dot(all_fig, all_cap.T, preferred_element_type=jnp.float32)
    row_lse = log_total(logits, 1)
    col_lse = log_total(logits, 0)
    eye_mat = jnp.eye(pair_total, dtype=jnp.float32)
    diag_logit = jnp.sum(logits * eye_mat, axis=1)
    own_rows = first_pair + jnp.arange(pair_count)
    own_mask = (jnp.arange(pair_total)[None, :] == own_rows[:, None]).astype(jnp.float32)
    loss_all = 0.5 * (row_lse - diag_logit) + 0.5 * (col_lse - diag_logit)
    pair_loss = jnp.dot(own_mask, loss_all, precision=lax.Precision.HIGHEST)
    prob_rows = jnp.exp(logits - row_lse[:, None])
    prob_cols = jnp.exp(logits - col_lse[None, :])
    coef = 0.5 * all_weight[:, None] * (prob_rows - eye_mat) + 0.5 * (
        prob_cols - eye_mat
    ) * all_weight[None, :]
    coef_rows = jnp.dot(own_mask, coef, precision=lax.Precision.HIGHEST)
    coef_cols = jnp.dot(own_mask, coef.T, precision=lax.Precision.HIGHEST)
    fig_grad = logit_mult * jnp.dot(
        coef_rows, all_cap.astype(jnp.float32), precision=lax.Precision.HIGHEST
    )
    cap_grad = logit_mult * jnp.dot(
        coef_cols, all_fig.astype(jnp.float32), precision=lax.Precision.HIGHEST
    )
    figure_direction = fig_inv * (
        fig_grad - fig_unit * jnp.sum(fig_unit * fig_grad, axis=1, keepdims=True)
    )
    caption_direction = cap_inv * (
        cap_grad - cap_unit * jnp.sum(cap_unit * cap_grad, axis=1, keepdims=True)
    )
    query_ct = jnp.concatenate([figure_direction, caption_direction], axis=0)
    query_ct_rows, key_value_ct = pullback(query_ct)
    half = feature_width // 2
    onehot_three = jnp.concatenate([query_onehot] * 3, axis=0)
    grad_parts = []
    for part in range(2):
        cols = slice(part * half, (part + 1) * half)
        query_part = lax.dot_general(
            query_ct_rows,
            qkv_full[0][cols],
            (((1,), (1,)), ((), ())),
            preferred_element_type=jnp.float32,
        )
        slot_part = lax.dot_general(
            key_value_ct,
            kv_full[cols],
            (((1,), (1,)), ((), ())),
            preferred_element_type=jnp.float32,
        )
        scatter_src = query_part + query_ct[:, cols]
        piece_hi = lax.reduce_precision(scatter_src, exponent_bits=8, mantissa_bits=7)
        rest = scatter_src - piece_hi
        piece_mid = lax.reduce_precision(rest, exponent_bits=8, mantissa_bits=7)
        piece_lo = rest - piece_mid
        pieces = jnp.concatenate([piece_hi, piece_mid, piece_lo], axis=0).astype(jnp.bfloat16)
        scatter_part = lax.dot_general(
            onehot_three,
            pieces,
            (((0,), (0,)), ((), ())),
            preferred_element_type=jnp.float32,
        )
        slot_gradient = (slot_part + scatter_part).astype(jnp.bfloat16)
        back_rows = jnp.einsum(
            "sop,sd->opd", recv_onehot, slot_gradient, preferred_element_type=jnp.float32
        ).astype(jnp.bfloat16)
        home_rows = lax.all_to_all(back_rows, "dp", split_axis=0, concat_axis=0, tiled=True)
        grad_parts.append(
            jnp.einsum(
                "opk,opd->kd", send_onehot, home_rows, preferred_element_type=jnp.float32
            ).astype(jnp.bfloat16)
        )
    page_grad = jnp.concatenate(grad_parts, axis=1)
    return (page_grad, pair_loss)


def solution(mesh):
    return jax.shard_map(
        body,
        mesh=mesh,
        in_specs=(
            P(("dp", "fsdp"), None),
            P(("dp", "fsdp")),
            P(("dp", "fsdp"), None),
            P(None, "fsdp", None),
            P(None, "fsdp"),
            P(("dp", "fsdp")),
            P(("dp", "fsdp")),
            P(),
            P(("dp", "fsdp")),
        ),
        out_specs=(P(("dp", "fsdp"), None), P(("dp", "fsdp"))),
        check_vma=False,
    )
```

```python
import math

import jax
import jax.numpy as jnp
from jax import lax
from jax.sharding import PartitionSpec as P

HD = 64


EPSILON = 1e-06


def log_total(values, axis):
    return jnp.log(jnp.sum(jnp.exp(values), axis=axis))


def attend(query_h, key_value, out_mat, query_doc, doc_row):
    query_count = query_h.shape[0]
    row_count = key_value.shape[0]
    head_width = query_h.shape[1]
    query_h = query_h.reshape(query_count, -1, HD)
    key_h = key_value[:, :head_width].reshape(row_count, -1, HD)
    value_h = key_value[:, head_width:].reshape(row_count, -1, HD)
    scores = jnp.einsum("qhd,khd->hqk", query_h, key_h, preferred_element_type=jnp.float32) * (
        1.0 / math.sqrt(HD)
    )
    same_doc = query_doc[:, None] == doc_row[None, :]
    scores = jnp.where(same_doc[None], scores, -1e30)
    weights = jnp.exp(scores)
    attn_prob = (weights / jnp.sum(weights, axis=2, keepdims=True)).astype(jnp.bfloat16)
    mixed = jnp.einsum("hqk,khd->qhd", attn_prob, value_h, preferred_element_type=jnp.float32)
    mixed = mixed.astype(jnp.bfloat16).reshape(query_count, -1)
    return jnp.dot(mixed, out_mat, preferred_element_type=jnp.float32)


def select_rows(onehot, rows):
    picked = jnp.dot(onehot, rows, preferred_element_type=jnp.float32)
    return picked.astype(rows.dtype)


def select_rows_t(onehot, rows):
    picked = lax.dot_general(
        onehot, rows, (((0,), (0,)), ((), ())), preferred_element_type=jnp.float32
    )
    return picked.astype(rows.dtype)


def body(
    page_embed,
    page_slot,
    doc_ids,
    qkv_weight,
    out_weight,
    fig_slot,
    cap_slot,
    logit_scale,
    loss_cotangent,
):
    dp_count = lax.axis_size("dp")
    row_count = page_embed.shape[0]
    feature_width = page_embed.shape[1]
    capacity = 5 * row_count // (4 * dp_count)
    buffer_rows = dp_count * capacity
    owner_idx = page_slot // row_count
    slot_idx = page_slot % row_count
    onehot = (owner_idx[:, None] == jnp.arange(dp_count)[None, :]).astype(jnp.int32)
    rank_idx = jnp.sum((jnp.cumsum(onehot, axis=0) - onehot) * onehot, axis=1)
    dest = owner_idx * capacity + rank_idx
    send_match = dest[None, :] == jnp.arange(buffer_rows)[:, None]
    send_ids = jnp.where(
        jnp.any(send_match, axis=1),
        jnp.sum(jnp.where(send_match, slot_idx[None, :], 0), axis=1),
        row_count,
    ).reshape(dp_count, capacity)
    send_onehot = jnp.concatenate(
        [
            send_match.astype(jnp.bfloat16).reshape(dp_count, capacity, row_count),
            jnp.zeros((dp_count, 1, row_count), jnp.bfloat16),
        ],
        axis=1,
    )
    id_lanes = jnp.zeros((dp_count, feature_width), jnp.float32)
    id_lanes = id_lanes.at[:, :capacity].set((send_ids // 16).astype(jnp.float32))
    id_lanes = id_lanes.at[:, 128 : 128 + capacity].set((send_ids % 16).astype(jnp.float32))
    id_rows = jnp.concatenate(
        [jnp.zeros((dp_count, capacity, feature_width), jnp.float32), id_lanes[:, None, :]], axis=1
    )
    send_rows = (
        jnp.einsum("opk,kd->opd", send_onehot, page_embed, preferred_element_type=jnp.float32)
        + id_rows
    ).astype(jnp.bfloat16)
    recv_rows = lax.all_to_all(send_rows, "dp", split_axis=0, concat_axis=0, tiled=True)
    id_row = recv_rows[:, capacity, :].astype(jnp.float32)
    recv_ids = (
        id_row[:, :capacity].astype(jnp.int32) * 16
        + id_row[:, 128 : 128 + capacity].astype(jnp.int32)
    )
    recv_ids = jnp.concatenate([recv_ids, jnp.full((dp_count, 1), row_count, jnp.int32)], axis=1)
    recv_onehot = (
        jnp.arange(row_count)[:, None, None] == recv_ids[None, :, :]
    ).astype(jnp.bfloat16)
    slot_row_block = jnp.einsum(
        "sop,opd->sd", recv_onehot, recv_rows, preferred_element_type=jnp.float32
    ).astype(jnp.bfloat16)
    qkv_full, out_full = (
        lax.all_gather(qkv_weight, "fsdp", axis=1, tiled=True),
        lax.all_gather(out_weight, "fsdp", axis=1, tiled=True),
    )
    kv_full = jnp.concatenate([qkv_full[1], qkv_full[2]], axis=1)
    doc_row = doc_ids[0]
    pair_count = fig_slot.shape[0]
    query_slots = jnp.concatenate([fig_slot, cap_slot], axis=0)
    query_onehot = (query_slots[:, None] == jnp.arange(row_count)[None, :]).astype(jnp.bfloat16)
    query_doc = jnp.sum(
        jnp.where(query_slots[:, None] == jnp.arange(row_count)[None, :], doc_row[None, :], 0),
        axis=1,
    )

    query_rows = select_rows(query_onehot, slot_row_block)
    query_h = jnp.dot(query_rows, qkv_full[0], preferred_element_type=jnp.float32).astype(
        jnp.bfloat16
    )
    key_value = jnp.dot(slot_row_block, kv_full, preferred_element_type=jnp.float32).astype(
        jnp.bfloat16
    )

    def branch(query_in, key_value_in):
        return attend(query_in, key_value_in, out_full, query_doc, doc_row)

    attn_out, pullback = jax.vjp(branch, query_h, key_value)
    query_output = query_rows.astype(jnp.float32) + attn_out
    fig_vec = query_output[:pair_count]
    cap_vec = query_output[pair_count:]
    fig_inv = lax.rsqrt(jnp.sum(fig_vec * fig_vec, axis=1, keepdims=True) + EPSILON)
    cap_inv = lax.rsqrt(jnp.sum(cap_vec * cap_vec, axis=1, keepdims=True) + EPSILON)
    fig_unit = fig_vec * fig_inv
    cap_unit = cap_vec * cap_inv
    fig_emb = fig_unit.astype(jnp.bfloat16)
    cap_emb = cap_unit.astype(jnp.bfloat16)
    weight_hi = loss_cotangent.astype(jnp.bfloat16)
    weight_lo = (loss_cotangent - weight_hi.astype(jnp.float32)).astype(jnp.bfloat16)
    weight_lanes = jnp.zeros((2 * pair_count, 128), jnp.bfloat16)
    weight_lanes = weight_lanes.at[:pair_count, 0].set(weight_hi).at[:pair_count, 1].set(weight_lo)
    both_emb = jnp.concatenate(
        [jnp.concatenate([fig_emb, cap_emb], axis=0), weight_lanes], axis=1
    )
    all_both = lax.all_to_all(
        jnp.broadcast_to(both_emb[None], (dp_count,) + both_emb.shape),
        "dp",
        split_axis=0,
        concat_axis=0,
        tiled=True,
    )
    all_fig = all_both[:, :pair_count, :feature_width].reshape(-1, feature_width)
    all_cap = all_both[:, pair_count:, :feature_width].reshape(-1, feature_width)
    all_weight = (
        all_both[:, :pair_count, feature_width].astype(jnp.float32)
        + all_both[:, :pair_count, feature_width + 1].astype(jnp.float32)
    ).reshape(-1)
    logit_mult = logit_scale[0]
    pair_total = all_fig.shape[0]
    first_pair = lax.axis_index("dp") * pair_count
    logits = logit_mult * jnp.dot(all_fig, all_cap.T, preferred_element_type=jnp.float32)
    row_lse = log_total(logits, 1)
    col_lse = log_total(logits, 0)
    eye_mat = jnp.eye(pair_total, dtype=jnp.float32)
    diag_logit = jnp.sum(logits * eye_mat, axis=1)
    own_rows = first_pair + jnp.arange(pair_count)
    own_mask = (jnp.arange(pair_total)[None, :] == own_rows[:, None]).astype(jnp.float32)
    loss_all = 0.5 * (row_lse - diag_logit) + 0.5 * (col_lse - diag_logit)
    pair_loss = lax.dynamic_slice(loss_all, (first_pair,), (pair_count,))
    prob_rows = jnp.exp(logits - row_lse[:, None])
    prob_cols = jnp.exp(logits - col_lse[None, :])
    coef = 0.5 * all_weight[:, None] * (prob_rows - eye_mat) + 0.5 * (
        prob_cols - eye_mat
    ) * all_weight[None, :]
    coef_rows = lax.dynamic_slice(coef, (first_pair, 0), (pair_count, pair_total))
    coef_cols = lax.dynamic_slice(coef, (0, first_pair), (pair_total, pair_count)).T

    def exact_product(coef_part, emb):
        piece_hi = lax.reduce_precision(coef_part, exponent_bits=8, mantissa_bits=7)
        rest = coef_part - piece_hi
        piece_mid = lax.reduce_precision(rest, exponent_bits=8, mantissa_bits=7)
        piece_lo = rest - piece_mid
        pieces = jnp.concatenate([piece_hi, piece_mid, piece_lo], axis=1).astype(jnp.bfloat16)
        emb_three = jnp.concatenate([emb, emb, emb], axis=0)
        return jnp.dot(pieces, emb_three, preferred_element_type=jnp.float32)

    fig_grad = logit_mult * exact_product(coef_rows, all_cap)
    cap_grad = logit_mult * exact_product(coef_cols, all_fig)
    figure_direction = fig_inv * (
        fig_grad - fig_unit * jnp.sum(fig_unit * fig_grad, axis=1, keepdims=True)
    )
    caption_direction = cap_inv * (
        cap_grad - cap_unit * jnp.sum(cap_unit * cap_grad, axis=1, keepdims=True)
    )
    query_ct = jnp.concatenate([figure_direction, caption_direction], axis=0)
    query_ct_rows, key_value_ct = pullback(query_ct)
    half = feature_width // 2
    onehot_three = jnp.concatenate([query_onehot] * 3, axis=0)
    grad_parts = []
    for part in range(2):
        cols = slice(part * half, (part + 1) * half)
        query_part = lax.dot_general(
            query_ct_rows,
            qkv_full[0][cols],
            (((1,), (1,)), ((), ())),
            preferred_element_type=jnp.float32,
        )
        slot_part = lax.dot_general(
            key_value_ct,
            kv_full[cols],
            (((1,), (1,)), ((), ())),
            preferred_element_type=jnp.float32,
        )
        scatter_src = query_part + query_ct[:, cols]
        piece_hi = lax.reduce_precision(scatter_src, exponent_bits=8, mantissa_bits=7)
        rest = scatter_src - piece_hi
        piece_mid = lax.reduce_precision(rest, exponent_bits=8, mantissa_bits=7)
        piece_lo = rest - piece_mid
        pieces = jnp.concatenate([piece_hi, piece_mid, piece_lo], axis=0).astype(jnp.bfloat16)
        scatter_part = lax.dot_general(
            onehot_three,
            pieces,
            (((0,), (0,)), ((), ())),
            preferred_element_type=jnp.float32,
        )
        slot_gradient = (slot_part + scatter_part).astype(jnp.bfloat16)
        back_rows = jnp.einsum(
            "sop,sd->opd", recv_onehot, slot_gradient, preferred_element_type=jnp.float32
        ).astype(jnp.bfloat16)
        home_rows = lax.all_to_all(back_rows, "dp", split_axis=0, concat_axis=0, tiled=True)
        grad_parts.append(
            jnp.einsum(
                "opk,opd->kd", send_onehot, home_rows, preferred_element_type=jnp.float32
            ).astype(jnp.bfloat16)
        )
    page_grad = jnp.concatenate(grad_parts, axis=1)
    return (page_grad, pair_loss)


def solution(mesh):
    return jax.shard_map(
        body,
        mesh=mesh,
        in_specs=(
            P(("dp", "fsdp"), None),
            P(("dp", "fsdp")),
            P(("dp", "fsdp"), None),
            P(None, "fsdp", None),
            P(None, "fsdp"),
            P(("dp", "fsdp")),
            P(("dp", "fsdp")),
            P(),
            P(("dp", "fsdp")),
        ),
        out_specs=(P(("dp", "fsdp"), None), P(("dp", "fsdp"))),
        check_vma=False,
    )
```

```python
import math

import jax
import jax.numpy as jnp
from jax import lax
from jax.sharding import PartitionSpec as P

HD = 64


EPSILON = 1e-06


def log_total(values, axis):
    return jnp.log(jnp.sum(jnp.exp(values), axis=axis))


def attend(query_h, key_value, out_mat, query_doc, doc_row):
    query_count = query_h.shape[0]
    row_count = key_value.shape[0]
    head_width = query_h.shape[1]
    query_h = query_h.reshape(query_count, -1, HD)
    key_h = key_value[:, :head_width].reshape(row_count, -1, HD)
    value_h = key_value[:, head_width:].reshape(row_count, -1, HD)
    scores = jnp.einsum("qhd,khd->hqk", query_h, key_h, preferred_element_type=jnp.float32) * (
        1.0 / math.sqrt(HD)
    )
    same_doc = query_doc[:, None] == doc_row[None, :]
    scores = jnp.where(same_doc[None], scores, -1e30)
    weights = jnp.exp(scores)
    attn_prob = (weights / jnp.sum(weights, axis=2, keepdims=True)).astype(jnp.bfloat16)
    mixed = jnp.einsum("hqk,khd->qhd", attn_prob, value_h, preferred_element_type=jnp.float32)
    mixed = mixed.astype(jnp.bfloat16).reshape(query_count, -1)
    return jnp.dot(mixed, out_mat, preferred_element_type=jnp.float32)


def select_rows(onehot, rows):
    picked = jnp.dot(onehot, rows, preferred_element_type=jnp.float32)
    return picked.astype(rows.dtype)


def select_rows_t(onehot, rows):
    picked = lax.dot_general(
        onehot, rows, (((0,), (0,)), ((), ())), preferred_element_type=jnp.float32
    )
    return picked.astype(rows.dtype)


def body(
    page_embed,
    page_slot,
    doc_ids,
    qkv_weight,
    out_weight,
    fig_slot,
    cap_slot,
    logit_scale,
    loss_cotangent,
):
    dp_count = lax.axis_size("dp")
    row_count = page_embed.shape[0]
    feature_width = page_embed.shape[1]
    capacity = 5 * row_count // (4 * dp_count)
    buffer_rows = dp_count * capacity
    owner_idx = page_slot // row_count
    slot_idx = page_slot % row_count
    onehot = (owner_idx[:, None] == jnp.arange(dp_count)[None, :]).astype(jnp.int32)
    rank_idx = jnp.sum((jnp.cumsum(onehot, axis=0) - onehot) * onehot, axis=1)
    dest = owner_idx * capacity + rank_idx
    send_match = dest[None, :] == jnp.arange(buffer_rows)[:, None]
    send_ids = jnp.where(
        jnp.any(send_match, axis=1),
        jnp.sum(jnp.where(send_match, slot_idx[None, :], 0), axis=1),
        row_count,
    ).reshape(dp_count, capacity)
    send_onehot = jnp.concatenate(
        [
            send_match.astype(jnp.bfloat16).reshape(dp_count, capacity, row_count),
            jnp.zeros((dp_count, 1, row_count), jnp.bfloat16),
        ],
        axis=1,
    )
    id_lanes = jnp.zeros((dp_count, feature_width), jnp.float32)
    id_lanes = id_lanes.at[:, :capacity].set((send_ids // 16).astype(jnp.float32))
    id_lanes = id_lanes.at[:, 128 : 128 + capacity].set((send_ids % 16).astype(jnp.float32))
    id_rows = jnp.concatenate(
        [jnp.zeros((dp_count, capacity, feature_width), jnp.float32), id_lanes[:, None, :]], axis=1
    )
    send_rows = (
        jnp.einsum("opk,kd->opd", send_onehot, page_embed, preferred_element_type=jnp.float32)
        + id_rows
    ).astype(jnp.bfloat16)
    recv_rows = lax.all_to_all(send_rows, "dp", split_axis=0, concat_axis=0, tiled=True)
    id_row = recv_rows[:, capacity, :].astype(jnp.float32)
    recv_ids = (
        id_row[:, :capacity].astype(jnp.int32) * 16
        + id_row[:, 128 : 128 + capacity].astype(jnp.int32)
    )
    recv_ids = jnp.concatenate([recv_ids, jnp.full((dp_count, 1), row_count, jnp.int32)], axis=1)
    recv_onehot = (
        jnp.arange(row_count)[:, None, None] == recv_ids[None, :, :]
    ).astype(jnp.bfloat16)
    slot_row_block = jnp.einsum(
        "sop,opd->sd", recv_onehot, recv_rows, preferred_element_type=jnp.float32
    ).astype(jnp.bfloat16)
    qkv_full, out_full = (
        lax.all_gather(qkv_weight, "fsdp", axis=1, tiled=True),
        lax.all_gather(out_weight, "fsdp", axis=1, tiled=True),
    )
    kv_full = jnp.concatenate([qkv_full[1], qkv_full[2]], axis=1)
    doc_row = doc_ids[0]
    pair_count = fig_slot.shape[0]
    query_slots = jnp.concatenate([fig_slot, cap_slot], axis=0)
    query_onehot = (query_slots[:, None] == jnp.arange(row_count)[None, :]).astype(jnp.bfloat16)
    query_doc = jnp.sum(
        jnp.where(query_slots[:, None] == jnp.arange(row_count)[None, :], doc_row[None, :], 0),
        axis=1,
    )

    query_rows = select_rows(query_onehot, slot_row_block)
    query_h = jnp.dot(query_rows, qkv_full[0], preferred_element_type=jnp.float32).astype(
        jnp.bfloat16
    )
    key_value = jnp.dot(slot_row_block, kv_full, preferred_element_type=jnp.float32).astype(
        jnp.bfloat16
    )

    def branch(query_in, key_value_in):
        return attend(query_in, key_value_in, out_full, query_doc, doc_row)

    attn_out, pullback = jax.vjp(branch, query_h, key_value)
    query_output = query_rows.astype(jnp.float32) + attn_out
    fig_vec = query_output[:pair_count]
    cap_vec = query_output[pair_count:]
    fig_inv = lax.rsqrt(jnp.sum(fig_vec * fig_vec, axis=1, keepdims=True) + EPSILON)
    cap_inv = lax.rsqrt(jnp.sum(cap_vec * cap_vec, axis=1, keepdims=True) + EPSILON)
    fig_unit = fig_vec * fig_inv
    cap_unit = cap_vec * cap_inv
    fig_emb = fig_unit.astype(jnp.bfloat16)
    cap_emb = cap_unit.astype(jnp.bfloat16)
    weight_hi = loss_cotangent.astype(jnp.bfloat16)
    weight_lo = (loss_cotangent - weight_hi.astype(jnp.float32)).astype(jnp.bfloat16)
    weight_lanes = jnp.zeros((2 * pair_count, 128), jnp.bfloat16)
    weight_lanes = weight_lanes.at[:pair_count, 0].set(weight_hi).at[:pair_count, 1].set(weight_lo)
    both_emb = jnp.concatenate(
        [jnp.concatenate([fig_emb, cap_emb], axis=0), weight_lanes], axis=1
    )
    all_both = lax.all_to_all(
        jnp.broadcast_to(both_emb[None], (dp_count,) + both_emb.shape),
        "dp",
        split_axis=0,
        concat_axis=0,
        tiled=True,
    )
    all_fig = all_both[:, :pair_count, :feature_width].reshape(-1, feature_width)
    all_cap = all_both[:, pair_count:, :feature_width].reshape(-1, feature_width)
    all_weight = (
        all_both[:, :pair_count, feature_width].astype(jnp.float32)
        + all_both[:, :pair_count, feature_width + 1].astype(jnp.float32)
    ).reshape(-1)
    logit_mult = logit_scale[0]
    pair_total = all_fig.shape[0]
    first_pair = lax.axis_index("dp") * pair_count
    logits = logit_mult * jnp.dot(all_fig, all_cap.T, preferred_element_type=jnp.float32)
    row_lse = log_total(logits, 1)
    col_lse = log_total(logits, 0)
    eye_mat = jnp.eye(pair_total, dtype=jnp.float32)
    diag_logit = jnp.sum(logits * eye_mat, axis=1)
    own_rows = first_pair + jnp.arange(pair_count)
    own_mask = (jnp.arange(pair_total)[None, :] == own_rows[:, None]).astype(jnp.float32)
    loss_all = 0.5 * (row_lse - diag_logit) + 0.5 * (col_lse - diag_logit)
    pair_loss = jnp.dot(own_mask, loss_all, precision=lax.Precision.HIGHEST)
    prob_rows = jnp.exp(logits - row_lse[:, None])
    prob_cols = jnp.exp(logits - col_lse[None, :])
    coef = 0.5 * all_weight[:, None] * (prob_rows - eye_mat) + 0.5 * (
        prob_cols - eye_mat
    ) * all_weight[None, :]
    coef_rows = jnp.dot(own_mask, coef, precision=lax.Precision.HIGHEST)
    coef_cols = jnp.dot(own_mask, coef.T, precision=lax.Precision.HIGHEST)
    def exact_product(coef_part, emb):
        piece_hi = lax.reduce_precision(coef_part, exponent_bits=8, mantissa_bits=7)
        rest = coef_part - piece_hi
        piece_mid = lax.reduce_precision(rest, exponent_bits=8, mantissa_bits=7)
        piece_lo = rest - piece_mid
        pieces = jnp.concatenate([piece_hi, piece_mid, piece_lo], axis=1).astype(jnp.bfloat16)
        emb_three = jnp.concatenate([emb, emb, emb], axis=0)
        return jnp.dot(pieces, emb_three, preferred_element_type=jnp.float32)

    fig_grad = logit_mult * exact_product(coef_rows, all_cap)
    cap_grad = logit_mult * exact_product(coef_cols, all_fig)
    figure_direction = fig_inv * (
        fig_grad - fig_unit * jnp.sum(fig_unit * fig_grad, axis=1, keepdims=True)
    )
    caption_direction = cap_inv * (
        cap_grad - cap_unit * jnp.sum(cap_unit * cap_grad, axis=1, keepdims=True)
    )
    query_ct = jnp.concatenate([figure_direction, caption_direction], axis=0)
    query_ct_rows, key_value_ct = pullback(query_ct)
    half = feature_width // 2
    onehot_three = jnp.concatenate([query_onehot] * 3, axis=0)
    grad_parts = []
    for part in range(2):
        cols = slice(part * half, (part + 1) * half)
        query_part = lax.dot_general(
            query_ct_rows,
            qkv_full[0][cols],
            (((1,), (1,)), ((), ())),
            preferred_element_type=jnp.float32,
        )
        slot_part = lax.dot_general(
            key_value_ct,
            kv_full[cols],
            (((1,), (1,)), ((), ())),
            preferred_element_type=jnp.float32,
        )
        scatter_src = query_part + query_ct[:, cols]
        piece_hi = lax.reduce_precision(scatter_src, exponent_bits=8, mantissa_bits=7)
        rest = scatter_src - piece_hi
        piece_mid = lax.reduce_precision(rest, exponent_bits=8, mantissa_bits=7)
        piece_lo = rest - piece_mid
        pieces = jnp.concatenate([piece_hi, piece_mid, piece_lo], axis=0).astype(jnp.bfloat16)
        scatter_part = lax.dot_general(
            onehot_three,
            pieces,
            (((0,), (0,)), ((), ())),
            preferred_element_type=jnp.float32,
        )
        slot_gradient = (slot_part + scatter_part).astype(jnp.bfloat16)
        back_rows = jnp.einsum(
            "sop,sd->opd", recv_onehot, slot_gradient, preferred_element_type=jnp.float32
        ).astype(jnp.bfloat16)
        home_rows = lax.all_to_all(back_rows, "dp", split_axis=0, concat_axis=0, tiled=True)
        grad_parts.append(
            jnp.einsum(
                "opk,opd->kd", send_onehot, home_rows, preferred_element_type=jnp.float32
            ).astype(jnp.bfloat16)
        )
    page_grad = jnp.concatenate(grad_parts, axis=1)
    return (page_grad, pair_loss)


def solution(mesh):
    return jax.shard_map(
        body,
        mesh=mesh,
        in_specs=(
            P(("dp", "fsdp"), None),
            P(("dp", "fsdp")),
            P(("dp", "fsdp"), None),
            P(None, "fsdp", None),
            P(None, "fsdp"),
            P(("dp", "fsdp")),
            P(("dp", "fsdp")),
            P(),
            P(("dp", "fsdp")),
        ),
        out_specs=(P(("dp", "fsdp"), None), P(("dp", "fsdp"))),
        check_vma=False,
    )
```
